256 devices in a mesh: req: 64 (over z, y, core), tp: 4 (over x).
Axes of the slice: x: 4, y: 4, z: 8, core: 2. Of those that a mesh axis runs over, the one named last changes fastest.
Arguments:
- tokens: bfloat16 [32768, 2048], P(('req', 'tp')), may hold values from -1000 to 1000
- query_weight: bfloat16 [2048, 2048], P(None, 'tp'), may hold values from -0.3125 to 0.3125
- kv_weight: bfloat16 [2048, 2, 2048], P(None, None, 'tp'), may hold values from -0.125 to 0.125
- out_weight: bfloat16 [2048, 2048], P('tp'), may hold values from -0.125 to 0.125
- cached_keys: bfloat16 [65536, 2048], P('req', 'tp'), may hold values from -70 to 70
- cached_values: bfloat16 [65536, 2048], P('req', 'tp'), may hold values from -6 to 6
- request_lengths: int32 [32], replicated, may hold values from 1 to 3, 64 in all
- group_order: int32 [64], replicated, may hold values from 0 to 63, each once
- group_offset: int32 [64], replicated, may hold values from 0 to 8191
- recompute_index: int32 [32768], P('req'), may hold values from 0 to 1023, as said below
Outputs:
- mixed: bfloat16 [32768, 2048], P(('req', 'tp'))
The draws below stay inside these ranges and needn't reach their ends.
Inputs may be any that keep to these rules, and one draw needn't show every extreme that they name: `request_lengths`: each request holds at least one group, they sum to 64, and some request holds exactly 3. `group_order`: every value appears once. `recompute_index`: the 512 positions of each group are distinct, increasing, and include 0 and 1023.
All inputs are finite; a program needn't handle non-finite values.
Results may differ from the reference program's by a relative error of at most 0.03.
Values may be sent and summed in bfloat16 or wider, within the bound.
No kernel may reach another device: no remote copies, remote signals or barrier semaphores. Data moves between devices by JAX's collectives and lax.ppermute only.
A program may use at most 128 MiB of HBM per device.

```python
import math
import jax
import jax.numpy as jnp
import numpy as np
from jax import lax

D = 2048
HEADS = 16
HEAD_DIM = 128
GROUP = 1024
MOST = 3
ANCHOR = 8192
RC_DEV = 512
N_GROUPS = 64
REQS = 32
TOKENS = 32768
CACHE = 65536


def draw_tokens(key, part):
    first_key, row_key, column_key = jax.random.split(key, 3)
    row_scale = jnp.exp(jax.random.uniform(row_key, (TOKENS, 1), minval=0.0, maxval=jnp.log(10.0)))
    column_scale = jnp.exp(jax.random.uniform(column_key, (1, D), minval=0.0, maxval=jnp.log(10.0)))
    base = jnp.clip(jax.random.normal(first_key, (TOKENS, D)), -6.0, 6.0)
    return (base * row_scale * column_scale).astype(jnp.bfloat16)


def draw_cached_keys(key, part):
    first_key = jax.random.fold_in(key, 0)
    feature_width = HEADS * HEAD_DIM
    base = jnp.clip(jax.random.normal(first_key, (CACHE, feature_width)), -6.0, 6.0)
    return base.astype(jnp.bfloat16)


def draw_recompute_index(key, part):

    def one_device(device_key):
        inner = jax.random.permutation(device_key, GROUP - 2)[:RC_DEV - 2] + 1
        picked = jnp.concatenate([jnp.zeros((1,), jnp.int32), inner.astype(jnp.int32), jnp.full((1,), GROUP - 1, jnp.int32)])
        return jnp.sort(picked)
    return jax.vmap(one_device)(jax.random.split(key, N_GROUPS)).reshape(N_GROUPS * RC_DEV)


def with_ends(drawn, stream_key, low, high):
    index_at = [jax.random.randint(jax.random.fold_in(stream_key, axis), (), 0, length) for axis, length in enumerate(drawn.shape)]
    widest = drawn.shape.index(max(drawn.shape))
    beside = index_at[:widest] + [(index_at[widest] + 1) % drawn.shape[widest]] + index_at[widest + 1:]
    return drawn.at[tuple(index_at)].set(low).at[tuple(beside)].set(high)


def block_scale(rng, shape, pieces, smallest, largest):
    loudness = 1.0
    for dim, shards_of in pieces:
        draws = jax.random.uniform(jax.random.fold_in(jax.random.fold_in(rng, 6), dim), (shards_of,), jnp.float32, smallest / len(pieces), largest / len(pieces))
        loudness = loudness * jnp.repeat(jnp.exp(draws), shape[dim] // shards_of).reshape((-1,) + (1,) * (len(shape) - 1 - dim))
    return loudness


def profile(count, total, bound, slope):
    portions = [(1 << 20) // math.isqrt(grade ** slope) + 1 for grade in range(2, count + 1)]
    surplus, counts = total - bound - (count - 1), [1] * (count - 1)
    while surplus > 0:
        candidates = [i for i in range(count - 1) if counts[i] < bound]
        whole, left = sum([portions[i] for i in candidates]), surplus
        for i in candidates:
            more = min(bound - counts[i], max(1, left * portions[i] // whole), surplus)
            counts[i] = counts[i] + more
            surplus = surplus - more
    return np.array([bound] + counts)


def ragged_sizes(rng, amount, total, most, slope):
    if amount == 2:
        one = jax.random.randint(rng, (), max(1, total - most), min(most, total - 1) + 1)
        return jnp.stack([one, total - one])
    lengths = jnp.asarray(profile(amount, total, most, slope), jnp.int32)
    pairs = (amount - 1) // 2
    giver, taker = lengths[1:1 + 2 * pairs:2], lengths[2:2 + 2 * pairs:2]
    room = jnp.minimum(giver - 1, most - taker)
    passed = jax.random.randint(jax.random.fold_in(rng, 1), (pairs,), 0, 1 << 20) % (room + 1)
    lengths = lengths.at[1:1 + 2 * pairs:2].set(giver - passed).at[2:2 + 2 * pairs:2].set(taker + passed)
    return lengths[jax.random.permutation(jax.random.fold_in(rng, 2), amount)]


def scatter_about(rng, dims, deviation, limit, pieces=(), kind=jnp.bfloat16):
    result = jax.random.normal(rng, dims, jnp.float32) * deviation
    if len(pieces) > 0:
        result = block_scale(rng, dims, pieces, -0.22, 0.18) * result
    return jnp.clip(result, min=-limit, max=limit).astype(kind)


def setup_inputs(seed: int = 0) -> dict:
    seeds = jax.random.split(jax.random.key(seed), 11)
    return {
        "tokens": draw_tokens(jax.random.fold_in(seeds[10], 71), 0),
        "query_weight": scatter_about(seeds[1], (D, HEADS * HEAD_DIM), 0.055, 0.3125, ((1, 4),)),
        "kv_weight": scatter_about(seeds[2], (D, 2, HEADS * HEAD_DIM), D ** -0.5, 0.125, ((2, 4),)),
        "out_weight": scatter_about(seeds[3], (HEADS * HEAD_DIM, D), (HEADS * HEAD_DIM) ** -0.5, 0.125, ((0, 4),)),
        "cached_keys": draw_cached_keys(jax.random.fold_in(seeds[10], 71), 0),
        "cached_values": scatter_about(seeds[5], (CACHE, HEADS * HEAD_DIM), 1.0, 6.0, ((0, 64), (1, 4))),
        "request_lengths": ragged_sizes(seeds[6], REQS, N_GROUPS, MOST, 2).astype(jnp.int32),
        "group_order": jax.random.permutation(seeds[7], N_GROUPS).astype(jnp.int32),
        "group_offset": with_ends(jax.random.randint(seeds[8], (N_GROUPS,), 0, ANCHOR), jax.random.fold_in(seeds[8], 1), 0, ANCHOR - 1).astype(jnp.int32),
        "recompute_index": draw_recompute_index(jax.random.fold_in(seeds[10], 71), 0),
    }


ROTARY_BASE = 10000.0
EPSILON = 1e-05
MASKED = -1e+30

def frequencies(half_dim):
    indices = jnp.arange(half_dim, dtype=jnp.float32)
    return jnp.exp(indices * (-jnp.log(jnp.float32(ROTARY_BASE)) / half_dim))

def rotate(vectors, angle_steps):
    half_dim = vectors.shape[-1] // 2
    angles = angle_steps[:, None, None] * frequencies(half_dim)[None, None, :]
    cosine = jnp.cos(angles)
    sine_part = jnp.sin(angles)
    first = vectors[..., :half_dim]
    second = vectors[..., half_dim:]
    return jnp.concatenate([first * cosine - second * sine_part, second * cosine + first * sine_part], axis=-1)

def group_layout(request_lengths, group_order):
    group_count = group_order.shape[0]
    request_ends = jnp.cumsum(request_lengths).astype(jnp.int32)
    group_ids = jnp.arange(group_count, dtype=jnp.int32)
    group_request = lax.optimization_barrier(jnp.sum((group_ids[:, None] >= request_ends[None, :]).astype(jnp.int32), axis=1))
    same_request = group_request[:, None] == group_request[None, :]
    earlier = group_order[None, :] < group_order[:, None]
    group_rank = lax.optimization_barrier(jnp.sum((same_request & earlier).astype(jnp.int32), axis=1))
    return (group_request, group_rank)

def layer_norm(rows_in):
    values32 = rows_in.astype(jnp.float32)
    row_mean = lax.optimization_barrier(jnp.mean(values32, axis=1, keepdims=True))
    centered = values32 - row_mean
    variance = lax.optimization_barrier(jnp.mean(centered * centered, axis=1, keepdims=True))
    return (centered * lax.rsqrt(variance + EPSILON)).astype(jnp.bfloat16)

def reference(tokens, query_weight, kv_weight, out_weight, cached_keys, cached_values, request_lengths, group_order, group_offset, recompute_index):
    feature_width = HEADS * HEAD_DIM
    group_count = group_order.shape[0]
    token_count = tokens.shape[0]
    cache_rows = cached_keys.shape[0]
    group_request, group_rank = group_layout(request_lengths, group_order)
    normalized = layer_norm(tokens)
    query_part = jnp.dot(normalized, query_weight, preferred_element_type=jnp.float32)
    kv_part = jnp.dot(normalized, kv_weight.reshape(D, 2 * feature_width), preferred_element_type=jnp.float32)
    row_group = (jnp.arange(token_count, dtype=jnp.int32) // RC_DEV).astype(jnp.int32)
    positions = (group_rank[row_group] * GROUP + recompute_index).astype(jnp.float32)
    queries = rotate(query_part.reshape(token_count, HEADS, HEAD_DIM), positions).reshape(token_count, feature_width).astype(jnp.bfloat16)
    fresh_keys = rotate(kv_part[:, :feature_width].reshape(token_count, HEADS, HEAD_DIM), positions).reshape(token_count, feature_width).astype(jnp.bfloat16)
    fresh_values = kv_part[:, feature_width:].astype(jnp.bfloat16)
    shifts = (group_rank * GROUP - group_offset).astype(jnp.float32)
    row_shift = jnp.repeat(shifts, GROUP)
    joined_keys = rotate(cached_keys.astype(jnp.float32).reshape(cache_rows, HEADS, HEAD_DIM), row_shift).reshape(cache_rows, feature_width).astype(jnp.bfloat16)
    target_rows = (row_group * GROUP + recompute_index).astype(jnp.int32)
    joined_keys = joined_keys.at[target_rows].set(fresh_keys)
    joined_values = cached_values.at[target_rows].set(fresh_values)
    reach = MOST - 1
    window = 2 * reach + 1
    padded_keys = jnp.pad(joined_keys, ((reach * GROUP, reach * GROUP), (0, 0)))
    padded_values = jnp.pad(joined_values, ((reach * GROUP, reach * GROUP), (0, 0)))
    padded_request = jnp.pad(group_request, (reach, reach), constant_values=-1)
    padded_rank = jnp.pad(group_rank, (reach, reach))
    key_position = jnp.arange(GROUP, dtype=jnp.int32)
    scale = HEAD_DIM ** (-0.5)

    def group_output(index):
        query_rows = lax.dynamic_slice_in_dim(queries, index * RC_DEV, RC_DEV, 0)
        query_index = lax.dynamic_slice_in_dim(recompute_index, index * RC_DEV, RC_DEV, 0)
        key_rows = lax.dynamic_slice_in_dim(padded_keys, index * GROUP, window * GROUP, 0)
        value_rows = lax.dynamic_slice_in_dim(padded_values, index * GROUP, window * GROUP, 0)
        near_request = lax.dynamic_slice_in_dim(padded_request, index, window, 0)
        near_rank = lax.dynamic_slice_in_dim(padded_rank, index, window, 0)
        own_request = group_request[index]
        own_rank = group_rank[index]
        earlier = (near_request == own_request) & (near_rank < own_rank)
        same_group = jnp.arange(window) == reach
        visible = earlier[None, :, None] | same_group[None, :, None] & (key_position[None, None, :] <= query_index[:, None, None])
        visible = visible.reshape(RC_DEV, window * GROUP)
        query_heads = query_rows.astype(jnp.float32).reshape(RC_DEV, HEADS, HEAD_DIM)
        key_heads = key_rows.astype(jnp.float32).reshape(window * GROUP, HEADS, HEAD_DIM)
        value_heads = value_rows.astype(jnp.float32).reshape(window * GROUP, HEADS, HEAD_DIM)
        scores = jnp.einsum('qhd,khd->hqk', query_heads, key_heads) * scale
        scores = jnp.where(visible[None], scores, MASKED)
        row_max = lax.optimization_barrier(jnp.max(scores, axis=2, keepdims=True))
        weights = jnp.where(visible[None], jnp.exp(scores - row_max), 0.0)
        denominator = lax.optimization_barrier(jnp.sum(weights, axis=2))
        rounded = lax.optimization_barrier(weights.astype(jnp.bfloat16)).astype(jnp.float32)
        numerator = jnp.einsum('hqk,khd->qhd', rounded, value_heads)
        return (numerator / jnp.transpose(denominator)[:, :, None]).reshape(RC_DEV, feature_width).astype(jnp.bfloat16)
    attention = lax.map(group_output, jnp.arange(group_count, dtype=jnp.int32)).reshape(token_count, feature_width)
    return jnp.dot(attention, out_weight, preferred_element_type=jnp.float32).astype(jnp.bfloat16)
```

```python
import jax
import jax.numpy as jnp
from jax import lax
from jax.sharding import PartitionSpec as P

HEAD_DIM = 128
GROUP = 1024
MOST = 3


ROTARY_BASE = 10000.0
EPSILON = 1e-05
MASKED = -1e30


def from_behind(x, axis, by):
    length = lax.axis_size(axis)
    pairs = [(i, i + by) for i in range(length) if 0 <= i + by < length]
    return lax.ppermute(x, axis, pairs)


def frequencies(half_dim):
    indices = jnp.arange(half_dim, dtype=jnp.float32)
    return jnp.exp(indices * (-jnp.log(jnp.float32(ROTARY_BASE)) / half_dim))


def rotate_with(vectors, cosine, sine_part):
    half_dim = vectors.shape[-1] // 2
    first = vectors[..., :half_dim]
    second = vectors[..., half_dim:]
    return jnp.concatenate(
        [first * cosine - second * sine_part, second * cosine + first * sine_part], axis=-1
    )


def group_layout(request_lengths, group_order):
    group_count = group_order.shape[0]
    request_ends = jnp.cumsum(request_lengths)
    group_ids = jnp.arange(group_count, dtype=jnp.int32)
    group_request = jnp.sum((group_ids[:, None] >= request_ends[None, :]).astype(jnp.int32), axis=1)
    same_request = group_request[:, None] == group_request[None, :]
    earlier = group_order[None, :] < group_order[:, None]
    group_rank = jnp.sum((same_request & earlier).astype(jnp.int32), axis=1)
    return (group_request, group_rank)


def layer_norm(rows_in):
    values32 = rows_in.astype(jnp.float32)
    row_mean = jnp.mean(values32, axis=1, keepdims=True)
    centered = values32 - row_mean
    variance = jnp.mean(centered * centered, axis=1, keepdims=True)
    return (centered * lax.rsqrt(variance + EPSILON)).astype(jnp.bfloat16)


def attend(queries, joined_keys, joined_values, visible):
    row_count = queries.shape[0]
    key_count = joined_keys.shape[0]
    head_count = queries.shape[1] // HEAD_DIM
    query_heads = queries.reshape(row_count, head_count, HEAD_DIM)
    key_heads = joined_keys.reshape(key_count, head_count, HEAD_DIM)
    value_heads = joined_values.reshape(key_count, head_count, HEAD_DIM)
    scores = jnp.einsum(
        "qhd,khd->hqk", query_heads, key_heads, preferred_element_type=jnp.float32
    ) * HEAD_DIM ** (-0.5)
    if visible is not None:
        scores = jnp.where(visible[None], scores, MASKED)
    row_max = jnp.max(scores, axis=2)
    weights = jnp.exp(scores - row_max[:, :, None])
    if visible is not None:
        weights = jnp.where(visible[None], weights, 0.0)
    denominator = jnp.sum(weights, axis=2)
    numerator = jnp.einsum(
        "hqk,khd->qhd",
        weights.astype(jnp.bfloat16),
        value_heads,
        preferred_element_type=jnp.float32,
    )
    return (numerator, row_max, denominator)


def combine(first, second):
    row_max = jnp.maximum(first[1], second[1])
    scale_first = jnp.exp(first[1] - row_max)
    scale_second = jnp.exp(second[1] - row_max)
    numerator = (
        first[0] * jnp.transpose(scale_first)[:, :, None]
        + second[0] * jnp.transpose(scale_second)[:, :, None]
    )
    denominator = first[2] * scale_first + second[2] * scale_second
    return (numerator, row_max, denominator)


def per_device(
    tokens,
    query_weight,
    kv_weight,
    out_weight,
    cached_keys,
    cached_values,
    request_lengths,
    group_order,
    group_offset,
    recompute_index,
):
    feature_width = query_weight.shape[1]
    head_count = feature_width // HEAD_DIM
    half_dim = HEAD_DIM // 2
    group_count = group_order.shape[0]
    device = lax.axis_index("req")
    group_request, group_rank = group_layout(request_lengths, group_order)
    own_request = group_request[device]
    own_rank = group_rank[device]
    full_out_weight = lax.all_gather(out_weight, "tp", axis=0, tiled=True)
    kv_columns = kv_weight.reshape(kv_weight.shape[0], 2 * feature_width)
    normalized = lax.all_gather(layer_norm(tokens), "tp", axis=0, tiled=True)
    query_part = jnp.dot(normalized, query_weight, preferred_element_type=jnp.float32)
    kv_part = jnp.dot(normalized, kv_columns, preferred_element_type=jnp.float32)
    row_count = query_part.shape[0]
    freq = frequencies(half_dim)
    positions = (own_rank * GROUP + recompute_index).astype(jnp.float32)
    angles = positions[:, None] * freq[None, :]
    row_cos = jnp.cos(angles)[:, None, :]
    row_sin = jnp.sin(angles)[:, None, :]
    queries = (
        rotate_with(query_part.reshape(row_count, head_count, HEAD_DIM), row_cos, row_sin)
        .reshape(row_count, feature_width)
        .astype(jnp.bfloat16)
    )
    fresh_keys = (
        rotate_with(
            kv_part[:, :feature_width].reshape(row_count, head_count, HEAD_DIM), row_cos, row_sin
        )
        .reshape(row_count, feature_width)
        .astype(jnp.bfloat16)
    )
    fresh_values = kv_part[:, feature_width:].astype(jnp.bfloat16)
    key_count = cached_keys.shape[0]
    rotation = (own_rank * GROUP - group_offset[device]).astype(jnp.float32)
    group_angles = rotation * freq
    group_cos = jnp.cos(group_angles)[None, None, :]
    group_sin = jnp.sin(group_angles)[None, None, :]
    rotated_keys = (
        rotate_with(
            cached_keys.astype(jnp.float32).reshape(key_count, head_count, HEAD_DIM),
            group_cos,
            group_sin,
        )
        .reshape(key_count, feature_width)
        .astype(jnp.bfloat16)
    )
    key_ids = jnp.arange(key_count, dtype=jnp.int32)
    placement = key_ids[:, None] == recompute_index[None, :]
    replaced = jnp.any(placement, axis=1)
    fresh_kv = jnp.concatenate([fresh_keys, fresh_values], axis=1)
    placed_kv = jnp.dot(
        placement.astype(jnp.bfloat16), fresh_kv, preferred_element_type=jnp.float32
    ).astype(jnp.bfloat16)
    cached_kv = jnp.concatenate([rotated_keys, cached_values], axis=1)
    joined_kv = jnp.where(replaced[:, None], placed_kv, cached_kv)
    joined_keys = joined_kv[:, :feature_width]
    joined_values = joined_kv[:, feature_width:]
    causal = key_ids[None, :] <= recompute_index[:, None]
    running = attend(queries, joined_keys, joined_values, causal)
    nothing = (
        jnp.zeros((row_count, head_count, HEAD_DIM), jnp.float32),
        jnp.full((head_count, row_count), MASKED, jnp.float32),
        jnp.zeros((head_count, row_count), jnp.float32),
    )
    distances = [distance for distance in range(1, MOST)] + [
        -distance for distance in range(1, MOST)
    ]
    for distance in distances:
        far_kv = from_behind(joined_kv, "req", distance)
        source_index = jnp.clip(device - distance, 0, group_count - 1)
        source_inside = (device - distance >= 0) & (device - distance < group_count)
        needed = (
            source_inside
            & (group_request[source_index] == own_request)
            & (group_rank[source_index] < own_rank)
        )
        partial_value = lax.cond(
            needed,
            lambda: attend(queries, far_kv[:, :feature_width], far_kv[:, feature_width:], None),
            lambda: nothing,
        )
        running = combine(running, partial_value)
    numerator, row_max, denominator = running
    attention = (
        (numerator / jnp.transpose(denominator)[:, :, None])
        .reshape(row_count, feature_width)
        .astype(jnp.bfloat16)
    )
    own_rows = lax.all_to_all(attention, "tp", 0, 1, tiled=True)
    return jnp.dot(own_rows, full_out_weight, preferred_element_type=jnp.float32).astype(
        jnp.bfloat16
    )


def solution(mesh):
    placed = (
        P(("req", "tp"), None),
        P(None, "tp"),
        P(None, None, "tp"),
        P("tp", None),
        P("req", "tp"),
        P("req", "tp"),
        P(),
        P(),
        P(),
        P("req"),
    )
    return jax.shard_map(
        per_device, mesh=mesh, in_specs=placed, out_specs=P(("req", "tp"), None), check_vma=False
    )
```

```python
import jax
import jax.numpy as jnp
from jax import lax
from jax.sharding import PartitionSpec as P

HEAD_DIM = 128
GROUP = 1024
MOST = 3


ROTARY_BASE = 10000.0
EPSILON = 1e-05
MASKED = -1e30


def from_behind(x, axis, by):
    length = lax.axis_size(axis)
    pairs = [(i, i + by) for i in range(length) if 0 <= i + by < length]
    return lax.ppermute(x, axis, pairs)


def frequencies(half_dim):
    indices = jnp.arange(half_dim, dtype=jnp.float32)
    return jnp.exp(indices * (-jnp.log(jnp.float32(ROTARY_BASE)) / half_dim))


def rotation_tables(angles, width):
    cosine = jnp.cos(angles)
    sine_part = jnp.sin(angles)
    repeats = width // (2 * angles.shape[-1])
    cos_full = jnp.tile(jnp.concatenate([cosine, cosine], axis=-1), (1, repeats))
    sin_full = jnp.tile(jnp.concatenate([-sine_part, sine_part], axis=-1), (1, repeats))
    return cos_full, sin_full


def rotate_flat(vectors, cos_full, sin_full):
    half_dim = HEAD_DIM // 2
    width = vectors.shape[-1]
    column = jnp.arange(width, dtype=jnp.int32) % HEAD_DIM
    partner = jnp.where(
        (column < half_dim)[None, :],
        jnp.roll(vectors, -half_dim, axis=1),
        jnp.roll(vectors, half_dim, axis=1),
    )
    return vectors * cos_full + partner * sin_full


def group_layout(request_lengths, group_order):
    group_count = group_order.shape[0]
    request_ends = jnp.cumsum(request_lengths)
    group_ids = jnp.arange(group_count, dtype=jnp.int32)
    group_request = jnp.sum((group_ids[:, None] >= request_ends[None, :]).astype(jnp.int32), axis=1)
    same_request = group_request[:, None] == group_request[None, :]
    earlier = group_order[None, :] < group_order[:, None]
    group_rank = jnp.sum((same_request & earlier).astype(jnp.int32), axis=1)
    return (group_request, group_rank)


def layer_norm(rows_in):
    values32 = rows_in.astype(jnp.float32)
    row_mean = jnp.mean(values32, axis=1, keepdims=True)
    centered = values32 - row_mean
    variance = jnp.mean(centered * centered, axis=1, keepdims=True)
    return (centered * lax.rsqrt(variance + EPSILON)).astype(jnp.bfloat16)


def attend(queries, joined_keys, joined_values, visible):
    row_count = queries.shape[0]
    key_count = joined_keys.shape[0]
    head_count = queries.shape[1] // HEAD_DIM
    query_heads = queries.reshape(row_count, head_count, HEAD_DIM)
    key_heads = joined_keys.reshape(key_count, head_count, HEAD_DIM)
    value_heads = joined_values.reshape(key_count, head_count, HEAD_DIM)
    scores = jnp.einsum(
        "qhd,khd->hqk", query_heads, key_heads, preferred_element_type=jnp.float32
    ) * HEAD_DIM ** (-0.5)
    if visible is not None:
        scores = jnp.where(visible[None], scores, MASKED)
    row_max = jnp.max(scores, axis=2)
    weights = jnp.exp(scores - row_max[:, :, None])
    if visible is not None:
        weights = jnp.where(visible[None], weights, 0.0)
    denominator = jnp.sum(weights, axis=2)
    numerator = jnp.einsum(
        "hqk,khd->qhd",
        weights.astype(jnp.bfloat16),
        value_heads,
        preferred_element_type=jnp.float32,
    )
    return (numerator, row_max, denominator)


def combine(first, second):
    row_max = jnp.maximum(first[1], second[1])
    scale_first = jnp.exp(first[1] - row_max)
    scale_second = jnp.exp(second[1] - row_max)
    numerator = (
        first[0] * jnp.transpose(scale_first)[:, :, None]
        + second[0] * jnp.transpose(scale_second)[:, :, None]
    )
    denominator = first[2] * scale_first + second[2] * scale_second
    return (numerator, row_max, denominator)


def per_device(
    tokens,
    query_weight,
    kv_weight,
    out_weight,
    cached_keys,
    cached_values,
    request_lengths,
    group_order,
    group_offset,
    recompute_index,
):
    feature_width = query_weight.shape[1]
    head_count = feature_width // HEAD_DIM
    half_dim = HEAD_DIM // 2
    group_count = group_order.shape[0]
    tp_size = lax.axis_size("tp")
    device = lax.axis_index("req")
    tp_index = lax.axis_index("tp")
    group_request, group_rank = group_layout(request_lengths, group_order)
    own_request = group_request[device]
    own_rank = group_rank[device]
    full_out_weight = lax.all_gather(out_weight, "tp", axis=0, tiled=True)
    freq = frequencies(half_dim)
    key_count = cached_keys.shape[0]
    row_count = recompute_index.shape[0]

    rotation = (own_rank * GROUP - group_offset[device]).astype(jnp.float32)
    group_cos, group_sin = rotation_tables((rotation * freq)[None, :], feature_width)
    rotated_keys = rotate_flat(cached_keys.astype(jnp.float32), group_cos, group_sin).astype(
        jnp.bfloat16
    )
    cached_kv = jnp.concatenate([rotated_keys, cached_values], axis=1)

    key_ids = jnp.arange(key_count, dtype=jnp.int32)
    placement = key_ids[:, None] == recompute_index[None, :]
    replaced = jnp.any(placement, axis=1)
    replaced_before = jnp.sum((recompute_index[None, :] < key_ids[:, None]).astype(jnp.int32), axis=1)
    kept_slot = key_ids - replaced_before
    packing = (~replaced)[None, :] & (
        jnp.arange(key_count - row_count, dtype=jnp.int32)[:, None] == kept_slot[None, :]
    )
    kept_kv = jnp.dot(
        packing.astype(jnp.bfloat16), cached_kv, preferred_element_type=jnp.float32
    ).astype(jnp.bfloat16)

    distances = [distance for distance in range(1, MOST)] + [
        -distance for distance in range(1, MOST)
    ]
    far_kept = [from_behind(kept_kv, "req", distance) for distance in distances]

    normalized = lax.all_gather(layer_norm(tokens), "tp", axis=0, tiled=True)
    query_part = jnp.dot(normalized, query_weight, preferred_element_type=jnp.float32)
    key_part = jnp.einsum(
        "nd,dc->nc", normalized, kv_weight[:, 0, :], preferred_element_type=jnp.float32
    )
    value_part = jnp.einsum(
        "nd,dc->nc", normalized, kv_weight[:, 1, :], preferred_element_type=jnp.float32
    )
    positions = (own_rank * GROUP + recompute_index).astype(jnp.float32)
    row_cos, row_sin = rotation_tables(positions[:, None] * freq[None, :], feature_width)
    queries = rotate_flat(query_part, row_cos, row_sin).astype(jnp.bfloat16)
    fresh_keys = rotate_flat(key_part, row_cos, row_sin).astype(jnp.bfloat16)
    fresh_values = value_part.astype(jnp.bfloat16)
    fresh_kv = jnp.concatenate([fresh_keys, fresh_values], axis=1)
    far_fresh = [from_behind(fresh_kv, "req", distance) for distance in distances]

    placed_kv = jnp.dot(
        placement.astype(jnp.bfloat16), fresh_kv, preferred_element_type=jnp.float32
    ).astype(jnp.bfloat16)
    joined_kv = jnp.where(replaced[:, None], placed_kv, cached_kv)
    causal = key_ids[None, :] <= recompute_index[:, None]
    running = attend(queries, joined_kv[:, :feature_width], joined_kv[:, feature_width:], causal)
    nothing = (
        jnp.zeros((row_count, head_count, HEAD_DIM), jnp.float32),
        jnp.full((head_count, row_count), MASKED, jnp.float32),
        jnp.zeros((head_count, row_count), jnp.float32),
    )
    for distance, kept_part, fresh_part in zip(distances, far_kept, far_fresh):
        source_index = jnp.clip(device - distance, 0, group_count - 1)
        source_inside = (device - distance >= 0) & (device - distance < group_count)
        needed = (
            source_inside
            & (group_request[source_index] == own_request)
            & (group_rank[source_index] < own_rank)
        )

        def far_attend(kept_part=kept_part, fresh_part=fresh_part):
            far_kv = jnp.concatenate([kept_part, fresh_part], axis=0)
            return attend(queries, far_kv[:, :feature_width], far_kv[:, feature_width:], None)

        partial_value = lax.cond(needed, far_attend, lambda: nothing)
        running = combine(running, partial_value)
    numerator, row_max, denominator = running
    attention = (
        (numerator / jnp.transpose(denominator)[:, :, None])
        .reshape(row_count, feature_width)
        .astype(jnp.bfloat16)
    )

    chunk = row_count // tp_size

    def rows_for(peer):
        return lax.dynamic_slice_in_dim(attention, peer * chunk, chunk, 0)

    def weight_of(peer):
        return lax.dynamic_slice_in_dim(full_out_weight, peer * feature_width, feature_width, 0)

    mixed = jnp.dot(rows_for(tp_index), weight_of(tp_index), preferred_element_type=jnp.float32)
    for shift in range(1, tp_size):
        pairs = [(peer, (peer + shift) % tp_size) for peer in range(tp_size)]
        arrived = lax.ppermute(rows_for((tp_index + shift) % tp_size), "tp", pairs)
        source = (tp_index - shift) % tp_size
        mixed = mixed + jnp.dot(arrived, weight_of(source), preferred_element_type=jnp.float32)
    return mixed.astype(jnp.bfloat16)


def solution(mesh):
    placed = (
        P(("req", "tp"), None),
        P(None, "tp"),
        P(None, None, "tp"),
        P("tp", None),
        P("req", "tp"),
        P("req", "tp"),
        P(),
        P(),
        P(),
        P("req"),
    )
    return jax.shard_map(
        per_device, mesh=mesh, in_specs=placed, out_specs=P(("req", "tp"), None), check_vma=False
    )
```

```python
import jax
import jax.numpy as jnp
from jax import lax
from jax.sharding import PartitionSpec as P
from jax.experimental import pallas as pl
from jax.experimental.pallas import tpu as pltpu

HEAD_DIM = 128
GROUP = 1024
MOST = 3


ROTARY_BASE = 10000.0
EPSILON = 1e-05
MASKED = -1e30


def from_behind(x, axis, by):
    length = lax.axis_size(axis)
    pairs = [(i, i + by) for i in range(length) if 0 <= i + by < length]
    return lax.ppermute(x, axis, pairs)


def frequencies(half_dim):
    indices = jnp.arange(half_dim, dtype=jnp.float32)
    return jnp.exp(indices * (-jnp.log(jnp.float32(ROTARY_BASE)) / half_dim))


def rotation_tables(angles, width):
    cosine = jnp.cos(angles)
    sine_part = jnp.sin(angles)
    repeats = width // (2 * angles.shape[-1])
    cos_full = jnp.tile(jnp.concatenate([cosine, cosine], axis=-1), (1, repeats))
    sin_full = jnp.tile(jnp.concatenate([-sine_part, sine_part], axis=-1), (1, repeats))
    return cos_full, sin_full


def rotate_flat(vectors, cos_full, sin_full):
    half_dim = HEAD_DIM // 2
    width = vectors.shape[-1]
    column = jnp.arange(width, dtype=jnp.int32) % HEAD_DIM
    partner = jnp.where(
        (column < half_dim)[None, :],
        jnp.roll(vectors, -half_dim, axis=1),
        jnp.roll(vectors, half_dim, axis=1),
    )
    return vectors * cos_full + partner * sin_full


def group_layout(request_lengths, group_order):
    group_count = group_order.shape[0]
    request_ends = jnp.cumsum(request_lengths)
    group_ids = jnp.arange(group_count, dtype=jnp.int32)
    group_request = jnp.sum((group_ids[:, None] >= request_ends[None, :]).astype(jnp.int32), axis=1)
    same_request = group_request[:, None] == group_request[None, :]
    earlier = group_order[None, :] < group_order[:, None]
    group_rank = jnp.sum((same_request & earlier).astype(jnp.int32), axis=1)
    return (group_request, group_rank)


def layer_norm(rows_in):
    values32 = rows_in.astype(jnp.float32)
    row_mean = jnp.mean(values32, axis=1, keepdims=True)
    centered = values32 - row_mean
    variance = jnp.mean(centered * centered, axis=1, keepdims=True)
    return (centered * lax.rsqrt(variance + EPSILON)).astype(jnp.bfloat16)


def attend(queries, joined_keys, joined_values, visible):
    row_count = queries.shape[0]
    key_count = joined_keys.shape[0]
    head_count = queries.shape[1] // HEAD_DIM
    query_heads = queries.reshape(row_count, head_count, HEAD_DIM)
    key_heads = joined_keys.reshape(key_count, head_count, HEAD_DIM)
    value_heads = joined_values.reshape(key_count, head_count, HEAD_DIM)
    scores = jnp.einsum(
        "qhd,khd->hqk", query_heads, key_heads, preferred_element_type=jnp.float32
    ) * HEAD_DIM ** (-0.5)
    if visible is not None:
        scores = jnp.where(visible[None], scores, MASKED)
    row_max = jnp.max(scores, axis=2)
    weights = jnp.exp(scores - row_max[:, :, None])
    if visible is not None:
        weights = jnp.where(visible[None], weights, 0.0)
    denominator = jnp.sum(weights, axis=2)
    numerator = jnp.einsum(
        "hqk,khd->qhd",
        weights.astype(jnp.bfloat16),
        value_heads,
        preferred_element_type=jnp.float32,
    )
    return (numerator, row_max, denominator)


def combine(first, second):
    row_max = jnp.maximum(first[1], second[1])
    scale_first = jnp.exp(first[1] - row_max)
    scale_second = jnp.exp(second[1] - row_max)
    numerator = (
        first[0] * jnp.transpose(scale_first)[:, :, None]
        + second[0] * jnp.transpose(scale_second)[:, :, None]
    )
    denominator = first[2] * scale_first + second[2] * scale_second
    return (numerator, row_max, denominator)


def attention_kernel(flags_ref, index_ref, query_ref, own_key_ref, own_value_ref, *refs):
    far_refs = refs[:-1]
    out_ref = refs[-1]
    scale = HEAD_DIM ** (-0.5)
    query = query_ref[...]
    scores = (
        lax.dot_general(
            query, own_key_ref[...], (((1,), (1,)), ((), ())), preferred_element_type=jnp.float32
        )
        * scale
    )
    key_ids = lax.broadcasted_iota(jnp.int32, scores.shape, 1)
    visible = key_ids <= index_ref[...]
    scores = jnp.where(visible, scores, MASKED)
    row_max = jnp.max(scores, axis=1, keepdims=True)
    weights = jnp.where(visible, jnp.exp(scores - row_max), 0.0)
    state = (
        row_max,
        jnp.sum(weights, axis=1, keepdims=True),
        jnp.dot(weights.astype(jnp.bfloat16), own_value_ref[...], preferred_element_type=jnp.float32),
    )
    slot_count = len(far_refs) // 4
    for slot in range(slot_count):
        kept_key, kept_value, fresh_key, fresh_value = far_refs[4 * slot : 4 * slot + 4]

        def block(key_ref, value_ref, carry):
            old_max, old_sum, old_acc = carry
            block_scores = (
                lax.dot_general(
                    query, key_ref[...], (((1,), (1,)), ((), ())),
                    preferred_element_type=jnp.float32,
                )
                * scale
            )
            new_max = jnp.maximum(old_max, jnp.max(block_scores, axis=1, keepdims=True))
            keep = jnp.exp(old_max - new_max)
            block_weights = jnp.exp(block_scores - new_max)
            return (
                new_max,
                keep * old_sum + jnp.sum(block_weights, axis=1, keepdims=True),
                keep * old_acc
                + jnp.dot(
                    block_weights.astype(jnp.bfloat16), value_ref[...],
                    preferred_element_type=jnp.float32,
                ),
            )

        def both(carry, kept_key=kept_key, kept_value=kept_value,
                 fresh_key=fresh_key, fresh_value=fresh_value):
            return block(fresh_key, fresh_value, block(kept_key, kept_value, carry))

        state = lax.cond(flags_ref[slot] != 0, both, lambda carry: carry, state)
    out_ref[...] = (state[2] / state[1]).astype(out_ref.dtype)


def fused_attention(flags, recompute_index, queries, joined_kv, far_parts):
    row_count, feature_width = queries.shape
    head_count = feature_width // HEAD_DIM
    key_count = joined_kv.shape[0]

    def column_spec(rows, offset, slot=None):
        if slot is None:
            return pl.BlockSpec((rows, HEAD_DIM), lambda h, flags_ref: (0, h + offset))
        return pl.BlockSpec(
            (rows, HEAD_DIM), lambda h, flags_ref: (0, (h + offset) * flags_ref[slot])
        )

    in_specs = [
        pl.BlockSpec((row_count, 1), lambda h, flags_ref: (0, 0)),
        column_spec(row_count, 0),
        column_spec(key_count, 0),
        column_spec(key_count, head_count),
    ]
    operands = [recompute_index.reshape(row_count, 1), queries, joined_kv, joined_kv]
    for slot, (kept_part, fresh_part) in enumerate(far_parts):
        in_specs += [
            column_spec(kept_part.shape[0], 0, slot),
            column_spec(kept_part.shape[0], head_count, slot),
            column_spec(fresh_part.shape[0], 0, slot),
            column_spec(fresh_part.shape[0], head_count, slot),
        ]
        operands += [kept_part, kept_part, fresh_part, fresh_part]
    grid_spec = pltpu.PrefetchScalarGridSpec(
        num_scalar_prefetch=1,
        grid=(head_count,),
        in_specs=in_specs,
        out_specs=pl.BlockSpec((row_count, HEAD_DIM), lambda h, flags_ref: (0, h)),
    )
    return pl.pallas_call(
        attention_kernel,
        grid_spec=grid_spec,
        out_shape=jax.ShapeDtypeStruct((row_count, feature_width), jnp.bfloat16),
        compiler_params=pltpu.CompilerParams(vmem_limit_bytes=48 * 1024 * 1024),
    )(flags, *operands)


def per_device(
    tokens,
    query_weight,
    kv_weight,
    out_weight,
    cached_keys,
    cached_values,
    request_lengths,
    group_order,
    group_offset,
    recompute_index,
):
    feature_width = query_weight.shape[1]
    head_count = feature_width // HEAD_DIM
    half_dim = HEAD_DIM // 2
    group_count = group_order.shape[0]
    tp_size = lax.axis_size("tp")
    device = lax.axis_index("req")
    tp_index = lax.axis_index("tp")
    group_request, group_rank = group_layout(request_lengths, group_order)
    own_request = group_request[device]
    own_rank = group_rank[device]
    full_out_weight = lax.all_gather(out_weight, "tp", axis=0, tiled=True)
    freq = frequencies(half_dim)
    key_count = cached_keys.shape[0]
    row_count = recompute_index.shape[0]

    rotation = (own_rank * GROUP - group_offset[device]).astype(jnp.float32)
    group_cos, group_sin = rotation_tables((rotation * freq)[None, :], feature_width)
    rotated_keys = rotate_flat(cached_keys.astype(jnp.float32), group_cos, group_sin).astype(
        jnp.bfloat16
    )
    cached_kv = jnp.concatenate([rotated_keys, cached_values], axis=1)

    key_ids = jnp.arange(key_count, dtype=jnp.int32)
    placement = key_ids[:, None] == recompute_index[None, :]
    replaced = jnp.any(placement, axis=1)
    replaced_before = jnp.sum((recompute_index[None, :] < key_ids[:, None]).astype(jnp.int32), axis=1)
    kept_slot = key_ids - replaced_before
    packing = (~replaced)[None, :] & (
        jnp.arange(key_count - row_count, dtype=jnp.int32)[:, None] == kept_slot[None, :]
    )
    kept_kv = jnp.dot(
        packing.astype(jnp.bfloat16), cached_kv, preferred_element_type=jnp.float32
    ).astype(jnp.bfloat16)

    distances = [distance for distance in range(1, MOST)] + [
        -distance for distance in range(1, MOST)
    ]
    far_kept = [from_behind(kept_kv, "req", distance) for distance in distances]

    normalized = lax.all_gather(layer_norm(tokens), "tp", axis=0, tiled=True)
    query_part = jnp.dot(normalized, query_weight, preferred_element_type=jnp.float32)
    key_part = jnp.einsum(
        "nd,dc->nc", normalized, kv_weight[:, 0, :], preferred_element_type=jnp.float32
    )
    value_part = jnp.einsum(
        "nd,dc->nc", normalized, kv_weight[:, 1, :], preferred_element_type=jnp.float32
    )
    positions = (own_rank * GROUP + recompute_index).astype(jnp.float32)
    row_cos, row_sin = rotation_tables(positions[:, None] * freq[None, :], feature_width)
    queries = rotate_flat(query_part, row_cos, row_sin).astype(jnp.bfloat16)
    fresh_keys = rotate_flat(key_part, row_cos, row_sin).astype(jnp.bfloat16)
    fresh_values = value_part.astype(jnp.bfloat16)
    fresh_kv = jnp.concatenate([fresh_keys, fresh_values], axis=1)
    far_fresh = [from_behind(fresh_kv, "req", distance) for distance in distances]

    placed_kv = jnp.dot(
        placement.astype(jnp.bfloat16), fresh_kv, preferred_element_type=jnp.float32
    ).astype(jnp.bfloat16)
    joined_kv = jnp.where(replaced[:, None], placed_kv, cached_kv)
    flags = []
    for distance in distances:
        source_index = jnp.clip(device - distance, 0, group_count - 1)
        source_inside = (device - distance >= 0) & (device - distance < group_count)
        needed = (
            source_inside
            & (group_request[source_index] == own_request)
            & (group_rank[source_index] < own_rank)
        )
        flags.append(needed.astype(jnp.int32))
    attention = fused_attention(
        jnp.stack(flags), recompute_index, queries, joined_kv, list(zip(far_kept, far_fresh))
    )

    chunk = row_count // tp_size

    def rows_for(peer):
        return lax.dynamic_slice_in_dim(attention, peer * chunk, chunk, 0)

    pieces = [rows_for(tp_index)]
    for shift in range(1, tp_size):
        pairs = [(peer, (peer + shift) % tp_size) for peer in range(tp_size)]
        pieces.append(lax.ppermute(rows_for((tp_index + shift) % tp_size), "tp", pairs))
    arrived = jnp.stack(pieces)
    own_rows = jnp.concatenate(
        [arrived[(tp_index - peer) % tp_size] for peer in range(tp_size)], axis=1
    )
    mixed = jnp.dot(own_rows, full_out_weight, preferred_element_type=jnp.float32)
    return mixed.astype(jnp.bfloat16)


def solution(mesh):
    placed = (
        P(("req", "tp"), None),
        P(None, "tp"),
        P(None, None, "tp"),
        P("tp", None),
        P("req", "tp"),
        P("req", "tp"),
        P(),
        P(),
        P(),
        P("req"),
    )
    return jax.shard_map(
        per_device, mesh=mesh, in_specs=placed, out_specs=P(("req", "tp"), None), check_vma=False
    )
```

```python
import jax
import jax.numpy as jnp
from jax import lax
from jax.sharding import PartitionSpec as P
from jax.experimental import pallas as pl
from jax.experimental.pallas import tpu as pltpu

HEAD_DIM = 128
GROUP = 1024
MOST = 3


ROTARY_BASE = 10000.0
EPSILON = 1e-05
MASKED = -1e30


def from_behind(x, axis, by):
    length = lax.axis_size(axis)
    pairs = [(i, i + by) for i in range(length) if 0 <= i + by < length]
    return lax.ppermute(x, axis, pairs)


def frequencies(half_dim):
    indices = jnp.arange(half_dim, dtype=jnp.float32)
    return jnp.exp(indices * (-jnp.log(jnp.float32(ROTARY_BASE)) / half_dim))


def rotation_tables(angles, width):
    cosine = jnp.cos(angles)
    sine_part = jnp.sin(angles)
    repeats = width // (2 * angles.shape[-1])
    cos_full = jnp.tile(jnp.concatenate([cosine, cosine], axis=-1), (1, repeats))
    sin_full = jnp.tile(jnp.concatenate([-sine_part, sine_part], axis=-1), (1, repeats))
    return cos_full, sin_full


def rotate_flat(vectors, cos_full, sin_full):
    half_dim = HEAD_DIM // 2
    width = vectors.shape[-1]
    column = jnp.arange(width, dtype=jnp.int32) % HEAD_DIM
    partner = jnp.where(
        (column < half_dim)[None, :],
        jnp.roll(vectors, -half_dim, axis=1),
        jnp.roll(vectors, half_dim, axis=1),
    )
    return vectors * cos_full + partner * sin_full


def group_layout(request_lengths, group_order):
    group_count = group_order.shape[0]
    request_ends = jnp.cumsum(request_lengths)
    group_ids = jnp.arange(group_count, dtype=jnp.int32)
    group_request = jnp.sum((group_ids[:, None] >= request_ends[None, :]).astype(jnp.int32), axis=1)
    same_request = group_request[:, None] == group_request[None, :]
    earlier = group_order[None, :] < group_order[:, None]
    group_rank = jnp.sum((same_request & earlier).astype(jnp.int32), axis=1)
    return (group_request, group_rank)


def layer_norm(rows_in):
    values32 = rows_in.astype(jnp.float32)
    row_mean = jnp.mean(values32, axis=1, keepdims=True)
    centered = values32 - row_mean
    variance = jnp.mean(centered * centered, axis=1, keepdims=True)
    return (centered * lax.rsqrt(variance + EPSILON)).astype(jnp.bfloat16)


def attend(queries, joined_keys, joined_values, visible):
    row_count = queries.shape[0]
    key_count = joined_keys.shape[0]
    head_count = queries.shape[1] // HEAD_DIM
    query_heads = queries.reshape(row_count, head_count, HEAD_DIM)
    key_heads = joined_keys.reshape(key_count, head_count, HEAD_DIM)
    value_heads = joined_values.reshape(key_count, head_count, HEAD_DIM)
    scores = jnp.einsum(
        "qhd,khd->hqk", query_heads, key_heads, preferred_element_type=jnp.float32
    ) * HEAD_DIM ** (-0.5)
    if visible is not None:
        scores = jnp.where(visible[None], scores, MASKED)
    row_max = jnp.max(scores, axis=2)
    weights = jnp.exp(scores - row_max[:, :, None])
    if visible is not None:
        weights = jnp.where(visible[None], weights, 0.0)
    denominator = jnp.sum(weights, axis=2)
    numerator = jnp.einsum(
        "hqk,khd->qhd",
        weights.astype(jnp.bfloat16),
        value_heads,
        preferred_element_type=jnp.float32,
    )
    return (numerator, row_max, denominator)


def combine(first, second):
    row_max = jnp.maximum(first[1], second[1])
    scale_first = jnp.exp(first[1] - row_max)
    scale_second = jnp.exp(second[1] - row_max)
    numerator = (
        first[0] * jnp.transpose(scale_first)[:, :, None]
        + second[0] * jnp.transpose(scale_second)[:, :, None]
    )
    denominator = first[2] * scale_first + second[2] * scale_second
    return (numerator, row_max, denominator)


def attention_kernel(flags_ref, index_ref, query_ref, own_key_ref, own_value_ref, *refs):
    far_refs = refs[:-1]
    out_ref = refs[-1]
    scale = HEAD_DIM ** (-0.5)
    query = query_ref[...]
    scores = (
        lax.dot_general(
            query, own_key_ref[...], (((1,), (1,)), ((), ())), preferred_element_type=jnp.float32
        )
        * scale
    )
    key_ids = lax.broadcasted_iota(jnp.int32, scores.shape, 1)
    visible = key_ids <= index_ref[...]
    scores = jnp.where(visible, scores, MASKED)
    row_max = jnp.max(scores, axis=1, keepdims=True)
    weights = jnp.where(visible, jnp.exp(scores - row_max), 0.0)
    state = (
        row_max,
        jnp.sum(weights, axis=1, keepdims=True),
        jnp.dot(weights.astype(jnp.bfloat16), own_value_ref[...], preferred_element_type=jnp.float32),
    )
    slot_count = len(far_refs) // 4
    for slot in range(slot_count):
        kept_key, kept_value, fresh_key, fresh_value = far_refs[4 * slot : 4 * slot + 4]

        def block(key_ref, value_ref, carry):
            old_max, old_sum, old_acc = carry
            block_scores = (
                lax.dot_general(
                    query, key_ref[...], (((1,), (1,)), ((), ())),
                    preferred_element_type=jnp.float32,
                )
                * scale
            )
            new_max = jnp.maximum(old_max, jnp.max(block_scores, axis=1, keepdims=True))
            keep = jnp.exp(old_max - new_max)
            block_weights = jnp.exp(block_scores - new_max)
            return (
                new_max,
                keep * old_sum + jnp.sum(block_weights, axis=1, keepdims=True),
                keep * old_acc
                + jnp.dot(
                    block_weights.astype(jnp.bfloat16), value_ref[...],
                    preferred_element_type=jnp.float32,
                ),
            )

        def both(carry, kept_key=kept_key, kept_value=kept_value,
                 fresh_key=fresh_key, fresh_value=fresh_value):
            return block(fresh_key, fresh_value, block(kept_key, kept_value, carry))

        state = lax.cond(flags_ref[slot] != 0, both, lambda carry: carry, state)
    out_ref[...] = (state[2] / state[1]).astype(out_ref.dtype)


def fused_attention(flags, recompute_index, queries, joined_kv, far_parts):
    row_count, feature_width = queries.shape
    head_count = feature_width // HEAD_DIM
    key_count = joined_kv.shape[0]

    def column_spec(rows, offset, slot=None):
        if slot is None:
            return pl.BlockSpec((rows, HEAD_DIM), lambda h, flags_ref: (0, h + offset))
        return pl.BlockSpec(
            (rows, HEAD_DIM), lambda h, flags_ref: (0, (h + offset) * flags_ref[slot])
        )

    in_specs = [
        pl.BlockSpec((row_count, 1), lambda h, flags_ref: (0, 0)),
        column_spec(row_count, 0),
        column_spec(key_count, 0),
        column_spec(key_count, head_count),
    ]
    operands = [recompute_index.reshape(row_count, 1), queries, joined_kv, joined_kv]
    for slot, (kept_part, fresh_part) in enumerate(far_parts):
        in_specs += [
            column_spec(kept_part.shape[0], 0, slot),
            column_spec(kept_part.shape[0], head_count, slot),
            column_spec(fresh_part.shape[0], 0, slot),
            column_spec(fresh_part.shape[0], head_count, slot),
        ]
        operands += [kept_part, kept_part, fresh_part, fresh_part]
    grid_spec = pltpu.PrefetchScalarGridSpec(
        num_scalar_prefetch=1,
        grid=(head_count,),
        in_specs=in_specs,
        out_specs=pl.BlockSpec((row_count, HEAD_DIM), lambda h, flags_ref: (0, h)),
    )
    return pl.pallas_call(
        attention_kernel,
        grid_spec=grid_spec,
        out_shape=jax.ShapeDtypeStruct((row_count, feature_width), jnp.bfloat16),
        compiler_params=pltpu.CompilerParams(vmem_limit_bytes=48 * 1024 * 1024),
    )(flags, *operands)


def per_device(
    tokens,
    query_weight,
    kv_weight,
    out_weight,
    cached_keys,
    cached_values,
    request_lengths,
    group_order,
    group_offset,
    recompute_index,
):
    feature_width = query_weight.shape[1]
    head_count = feature_width // HEAD_DIM
    half_dim = HEAD_DIM // 2
    group_count = group_order.shape[0]
    tp_size = lax.axis_size("tp")
    device = lax.axis_index("req")
    tp_index = lax.axis_index("tp")
    group_request, group_rank = group_layout(request_lengths, group_order)
    own_request = group_request[device]
    own_rank = group_rank[device]
    core = device % 2
    half_width = out_weight.shape[1] // 2
    mine_half = lax.all_gather(
        lax.dynamic_slice_in_dim(out_weight, core * half_width, half_width, 1), "tp", axis=0, tiled=True
    )
    req_size = lax.axis_size("req")
    sibling = [(i, i ^ 1) for i in range(req_size)]
    freq = frequencies(half_dim)
    key_count = cached_keys.shape[0]
    row_count = recompute_index.shape[0]

    rotation = (own_rank * GROUP - group_offset[device]).astype(jnp.float32)
    group_cos, group_sin = rotation_tables((rotation * freq)[None, :], feature_width)
    rotated_keys = rotate_flat(cached_keys.astype(jnp.float32), group_cos, group_sin).astype(
        jnp.bfloat16
    )
    cached_kv = jnp.concatenate([rotated_keys, cached_values], axis=1)

    key_ids = jnp.arange(key_count, dtype=jnp.int32)
    placement = key_ids[:, None] == recompute_index[None, :]
    replaced = jnp.any(placement, axis=1)
    replaced_before = jnp.sum((recompute_index[None, :] < key_ids[:, None]).astype(jnp.int32), axis=1)
    kept_slot = key_ids - replaced_before
    packing = (~replaced)[None, :] & (
        jnp.arange(key_count - row_count, dtype=jnp.int32)[:, None] == kept_slot[None, :]
    )
    kept_kv = jnp.dot(
        packing.astype(jnp.bfloat16), cached_kv, preferred_element_type=jnp.float32
    ).astype(jnp.bfloat16)

    distances = [distance for distance in range(1, MOST)] + [
        -distance for distance in range(1, MOST)
    ]
    far_kept = [from_behind(kept_kv, "req", distance) for distance in distances]

    normalized = lax.all_gather(layer_norm(tokens), "tp", axis=0, tiled=True)
    query_part = jnp.dot(normalized, query_weight, preferred_element_type=jnp.float32)
    kv_part = jnp.einsum("nd,dkc->knc", normalized, kv_weight, preferred_element_type=jnp.float32)
    key_part = kv_part[0]
    value_part = kv_part[1]
    positions = (own_rank * GROUP + recompute_index).astype(jnp.float32)
    row_cos, row_sin = rotation_tables(positions[:, None] * freq[None, :], feature_width)
    queries = rotate_flat(query_part, row_cos, row_sin).astype(jnp.bfloat16)
    fresh_keys = rotate_flat(key_part, row_cos, row_sin).astype(jnp.bfloat16)
    fresh_values = value_part.astype(jnp.bfloat16)
    fresh_kv = jnp.concatenate([fresh_keys, fresh_values], axis=1)
    far_fresh = [from_behind(fresh_kv, "req", distance) for distance in distances]

    placed_kv = jnp.dot(
        placement.astype(jnp.bfloat16), fresh_kv, preferred_element_type=jnp.float32
    ).astype(jnp.bfloat16)
    joined_kv = jnp.where(replaced[:, None], placed_kv, cached_kv)
    flags = []
    for distance in distances:
        source_index = jnp.clip(device - distance, 0, group_count - 1)
        source_inside = (device - distance >= 0) & (device - distance < group_count)
        needed = (
            source_inside
            & (group_request[source_index] == own_request)
            & (group_rank[source_index] < own_rank)
        )
        flags.append(needed.astype(jnp.int32))
    attention = fused_attention(
        jnp.stack(flags), recompute_index, queries, joined_kv, list(zip(far_kept, far_fresh))
    )

    chunk = row_count // tp_size

    def rows_for(peer):
        return lax.dynamic_slice_in_dim(attention, peer * chunk, chunk, 0)

    pieces = [rows_for(tp_index)]
    for shift in range(1, tp_size):
        pairs = [(peer, (peer + shift) % tp_size) for peer in range(tp_size)]
        pieces.append(lax.ppermute(rows_for((tp_index + shift) % tp_size), "tp", pairs))
    arrived = jnp.stack(pieces)
    own_rows = jnp.concatenate(
        [arrived[(tp_index - peer) % tp_size] for peer in range(tp_size)], axis=1
    )
    sibling_rows = lax.ppermute(own_rows, "req", sibling)
    both_rows = jnp.concatenate([own_rows, sibling_rows], axis=0)
    both_mixed = jnp.dot(both_rows, mine_half, preferred_element_type=jnp.float32).astype(jnp.bfloat16)
    chunk_rows = own_rows.shape[0]
    mixed_mine = both_mixed[:chunk_rows]
    mixed_other = lax.ppermute(both_mixed[chunk_rows:], "req", sibling)
    return jnp.where(
        core == 0,
        jnp.concatenate([mixed_mine, mixed_other], axis=1),
        jnp.concatenate([mixed_other, mixed_mine], axis=1),
    )


def solution(mesh):
    placed = (
        P(("req", "tp"), None),
        P(None, "tp"),
        P(None, None, "tp"),
        P("tp", None),
        P("req", "tp"),
        P("req", "tp"),
        P(),
        P(),
        P(),
        P("req"),
    )
    return jax.shard_map(
        per_device, mesh=mesh, in_specs=placed, out_specs=P(("req", "tp"), None), check_vma=False
    )
```

```python
import jax
import jax.numpy as jnp
from jax import lax
from jax.sharding import PartitionSpec as P
from jax.experimental import pallas as pl
from jax.experimental.pallas import tpu as pltpu

HEAD_DIM = 128
GROUP = 1024
MOST = 3


ROTARY_BASE = 10000.0
EPSILON = 1e-05
MASKED = -1e30


def from_behind(x, axis, by):
    length = lax.axis_size(axis)
    pairs = [(i, i + by) for i in range(length) if 0 <= i + by < length]
    return lax.ppermute(x, axis, pairs)


def frequencies(half_dim):
    indices = jnp.arange(half_dim, dtype=jnp.float32)
    return jnp.exp(indices * (-jnp.log(jnp.float32(ROTARY_BASE)) / half_dim))


def rotation_tables(angles, width):
    cosine = jnp.cos(angles)
    sine_part = jnp.sin(angles)
    repeats = width // (2 * angles.shape[-1])
    cos_full = jnp.tile(jnp.concatenate([cosine, cosine], axis=-1), (1, repeats))
    sin_full = jnp.tile(jnp.concatenate([-sine_part, sine_part], axis=-1), (1, repeats))
    return cos_full, sin_full


def rotate_flat(vectors, cos_full, sin_full):
    half_dim = HEAD_DIM // 2
    width = vectors.shape[-1]
    column = jnp.arange(width, dtype=jnp.int32) % HEAD_DIM
    partner = jnp.where(
        (column < half_dim)[None, :],
        jnp.roll(vectors, -half_dim, axis=1),
        jnp.roll(vectors, half_dim, axis=1),
    )
    return vectors * cos_full + partner * sin_full


def group_layout(request_lengths, group_order):
    group_count = group_order.shape[0]
    request_ends = jnp.cumsum(request_lengths)
    group_ids = jnp.arange(group_count, dtype=jnp.int32)
    group_request = jnp.sum((group_ids[:, None] >= request_ends[None, :]).astype(jnp.int32), axis=1)
    same_request = group_request[:, None] == group_request[None, :]
    earlier = group_order[None, :] < group_order[:, None]
    group_rank = jnp.sum((same_request & earlier).astype(jnp.int32), axis=1)
    return (group_request, group_rank)


def layer_norm(rows_in):
    values32 = rows_in.astype(jnp.float32)
    row_mean = jnp.mean(values32, axis=1, keepdims=True)
    centered = values32 - row_mean
    variance = jnp.mean(centered * centered, axis=1, keepdims=True)
    return (centered * lax.rsqrt(variance + EPSILON)).astype(jnp.bfloat16)


def attend(queries, joined_keys, joined_values, visible):
    row_count = queries.shape[0]
    key_count = joined_keys.shape[0]
    head_count = queries.shape[1] // HEAD_DIM
    query_heads = queries.reshape(row_count, head_count, HEAD_DIM)
    key_heads = joined_keys.reshape(key_count, head_count, HEAD_DIM)
    value_heads = joined_values.reshape(key_count, head_count, HEAD_DIM)
    scores = jnp.einsum(
        "qhd,khd->hqk", query_heads, key_heads, preferred_element_type=jnp.float32
    ) * HEAD_DIM ** (-0.5)
    if visible is not None:
        scores = jnp.where(visible[None], scores, MASKED)
    row_max = jnp.max(scores, axis=2)
    weights = jnp.exp(scores - row_max[:, :, None])
    if visible is not None:
        weights = jnp.where(visible[None], weights, 0.0)
    denominator = jnp.sum(weights, axis=2)
    numerator = jnp.einsum(
        "hqk,khd->qhd",
        weights.astype(jnp.bfloat16),
        value_heads,
        preferred_element_type=jnp.float32,
    )
    return (numerator, row_max, denominator)


def combine(first, second):
    row_max = jnp.maximum(first[1], second[1])
    scale_first = jnp.exp(first[1] - row_max)
    scale_second = jnp.exp(second[1] - row_max)
    numerator = (
        first[0] * jnp.transpose(scale_first)[:, :, None]
        + second[0] * jnp.transpose(scale_second)[:, :, None]
    )
    denominator = first[2] * scale_first + second[2] * scale_second
    return (numerator, row_max, denominator)


def attention_kernel(flags_ref, index_ref, query_ref, own_key_ref, own_value_ref, *refs):
    far_refs = refs[:-1]
    out_ref = refs[-1]
    scale = HEAD_DIM ** (-0.5)
    query = query_ref[...]
    scores = (
        lax.dot_general(
            query, own_key_ref[...], (((1,), (1,)), ((), ())), preferred_element_type=jnp.float32
        )
        * scale
    )
    key_ids = lax.broadcasted_iota(jnp.int32, scores.shape, 1)
    visible = key_ids <= index_ref[...]
    scores = jnp.where(visible, scores, MASKED)
    row_max = jnp.max(scores, axis=1, keepdims=True)
    weights = jnp.where(visible, jnp.exp(scores - row_max), 0.0)
    state = (
        row_max,
        jnp.sum(weights, axis=1, keepdims=True),
        jnp.dot(weights.astype(jnp.bfloat16), own_value_ref[...], preferred_element_type=jnp.float32),
    )
    slot_count = len(far_refs) // 4
    for slot in range(slot_count):
        kept_key, kept_value, fresh_key, fresh_value = far_refs[4 * slot : 4 * slot + 4]

        def block(key_ref, value_ref, carry):
            old_max, old_sum, old_acc = carry
            block_scores = (
                lax.dot_general(
                    query, key_ref[...], (((1,), (1,)), ((), ())),
                    preferred_element_type=jnp.float32,
                )
                * scale
            )
            new_max = jnp.maximum(old_max, jnp.max(block_scores, axis=1, keepdims=True))
            keep = jnp.exp(old_max - new_max)
            block_weights = jnp.exp(block_scores - new_max)
            return (
                new_max,
                keep * old_sum + jnp.sum(block_weights, axis=1, keepdims=True),
                keep * old_acc
                + jnp.dot(
                    block_weights.astype(jnp.bfloat16), value_ref[...],
                    preferred_element_type=jnp.float32,
                ),
            )

        def both(carry, kept_key=kept_key, kept_value=kept_value,
                 fresh_key=fresh_key, fresh_value=fresh_value):
            return block(fresh_key, fresh_value, block(kept_key, kept_value, carry))

        state = lax.cond(flags_ref[slot] != 0, both, lambda carry: carry, state)
    out_ref[...] = (state[2] / state[1]).astype(out_ref.dtype)


def fused_attention(flags, recompute_index, queries, joined_kv, far_parts):
    row_count, feature_width = queries.shape
    head_count = feature_width // HEAD_DIM
    key_count = joined_kv.shape[0]

    def column_spec(rows, offset, slot=None):
        if slot is None:
            return pl.BlockSpec((rows, HEAD_DIM), lambda h, flags_ref: (0, h + offset))
        return pl.BlockSpec(
            (rows, HEAD_DIM), lambda h, flags_ref: (0, (h + offset) * flags_ref[slot])
        )

    in_specs = [
        pl.BlockSpec((row_count, 1), lambda h, flags_ref: (0, 0)),
        column_spec(row_count, 0),
        column_spec(key_count, 0),
        column_spec(key_count, head_count),
    ]
    operands = [recompute_index.reshape(row_count, 1), queries, joined_kv, joined_kv]
    for slot, (kept_part, fresh_part) in enumerate(far_parts):
        in_specs += [
            column_spec(kept_part.shape[0], 0, slot),
            column_spec(kept_part.shape[0], head_count, slot),
            column_spec(fresh_part.shape[0], 0, slot),
            column_spec(fresh_part.shape[0], head_count, slot),
        ]
        operands += [kept_part, kept_part, fresh_part, fresh_part]
    grid_spec = pltpu.PrefetchScalarGridSpec(
        num_scalar_prefetch=1,
        grid=(head_count,),
        in_specs=in_specs,
        out_specs=pl.BlockSpec((row_count, HEAD_DIM), lambda h, flags_ref: (0, h)),
    )
    return pl.pallas_call(
        attention_kernel,
        grid_spec=grid_spec,
        out_shape=jax.ShapeDtypeStruct((row_count, feature_width), jnp.bfloat16),
        compiler_params=pltpu.CompilerParams(vmem_limit_bytes=48 * 1024 * 1024),
    )(flags, *operands)


def per_device(
    tokens,
    query_weight,
    kv_weight,
    out_weight,
    cached_keys,
    cached_values,
    request_lengths,
    group_order,
    group_offset,
    recompute_index,
):
    feature_width = query_weight.shape[1]
    head_count = feature_width // HEAD_DIM
    half_dim = HEAD_DIM // 2
    group_count = group_order.shape[0]
    tp_size = lax.axis_size("tp")
    device = lax.axis_index("req")
    tp_index = lax.axis_index("tp")
    group_request, group_rank = group_layout(request_lengths, group_order)
    own_request = group_request[device]
    own_rank = group_rank[device]
    core = device % 2
    half_width = out_weight.shape[1] // 2
    req_size = lax.axis_size("req")
    sibling = [(i, i ^ 1) for i in range(req_size)]
    freq = frequencies(half_dim)
    key_count = cached_keys.shape[0]
    row_count = recompute_index.shape[0]

    rotation = (own_rank * GROUP - group_offset[device]).astype(jnp.float32)
    group_cos, group_sin = rotation_tables((rotation * freq)[None, :], feature_width)
    rotated_keys = rotate_flat(cached_keys.astype(jnp.float32), group_cos, group_sin).astype(
        jnp.bfloat16
    )
    cached_kv = jnp.concatenate([rotated_keys, cached_values], axis=1)

    key_ids = jnp.arange(key_count, dtype=jnp.int32)
    placement = key_ids[:, None] == recompute_index[None, :]
    replaced = jnp.any(placement, axis=1)
    replaced_before = jnp.sum((recompute_index[None, :] < key_ids[:, None]).astype(jnp.int32), axis=1)
    kept_slot = key_ids - replaced_before
    packing = (~replaced)[None, :] & (
        jnp.arange(key_count - row_count, dtype=jnp.int32)[:, None] == kept_slot[None, :]
    )
    kept_kv = jnp.dot(
        packing.astype(jnp.bfloat16), cached_kv, preferred_element_type=jnp.float32
    ).astype(jnp.bfloat16)

    distances = [distance for distance in range(1, MOST)] + [
        -distance for distance in range(1, MOST)
    ]
    far_kept = [from_behind(kept_kv, "req", distance) for distance in distances]

    normalized = lax.all_gather(layer_norm(tokens), "tp", axis=0, tiled=True)
    normalized, weight_slice = lax.optimization_barrier(
        (normalized, lax.dynamic_slice_in_dim(out_weight, core * half_width, half_width, 1))
    )
    mine_half = lax.all_gather(weight_slice, "tp", axis=0, tiled=True)
    query_part = jnp.dot(normalized, query_weight, preferred_element_type=jnp.float32)
    kv_part = jnp.einsum("nd,dkc->knc", normalized, kv_weight, preferred_element_type=jnp.float32)
    key_part = kv_part[0]
    value_part = kv_part[1]
    positions = (own_rank * GROUP + recompute_index).astype(jnp.float32)
    row_cos, row_sin = rotation_tables(positions[:, None] * freq[None, :], feature_width)
    queries = rotate_flat(query_part, row_cos, row_sin).astype(jnp.bfloat16)
    fresh_keys = rotate_flat(key_part, row_cos, row_sin).astype(jnp.bfloat16)
    fresh_values = value_part.astype(jnp.bfloat16)
    fresh_kv = jnp.concatenate([fresh_keys, fresh_values], axis=1)
    far_fresh = [from_behind(fresh_kv, "req", distance) for distance in distances]

    placed_kv = jnp.dot(
        placement.astype(jnp.bfloat16), fresh_kv, preferred_element_type=jnp.float32
    ).astype(jnp.bfloat16)
    joined_kv = jnp.where(replaced[:, None], placed_kv, cached_kv)
    flags = []
    for distance in distances:
        source_index = jnp.clip(device - distance, 0, group_count - 1)
        source_inside = (device - distance >= 0) & (device - distance < group_count)
        needed = (
            source_inside
            & (group_request[source_index] == own_request)
            & (group_rank[source_index] < own_rank)
        )
        flags.append(needed.astype(jnp.int32))
    attention = fused_attention(
        jnp.stack(flags), recompute_index, queries, joined_kv, list(zip(far_kept, far_fresh))
    )

    chunk = row_count // tp_size

    def rows_for(peer):
        return lax.dynamic_slice_in_dim(attention, peer * chunk, chunk, 0)

    pieces = [rows_for(tp_index)]
    for shift in range(1, tp_size):
        pairs = [(peer, (peer + shift) % tp_size) for peer in range(tp_size)]
        pieces.append(lax.ppermute(rows_for((tp_index + shift) % tp_size), "tp", pairs))
    arrived = jnp.stack(pieces)
    own_rows = jnp.concatenate(
        [arrived[(tp_index - peer) % tp_size] for peer in range(tp_size)], axis=1
    )
    sibling_rows = lax.ppermute(own_rows, "req", sibling)
    both_rows = jnp.concatenate([own_rows, sibling_rows], axis=0)
    both_mixed = jnp.dot(both_rows, mine_half, preferred_element_type=jnp.float32).astype(jnp.bfloat16)
    chunk_rows = own_rows.shape[0]
    mixed_mine = both_mixed[:chunk_rows]
    mixed_other = lax.ppermute(both_mixed[chunk_rows:], "req", sibling)
    return jnp.where(
        core == 0,
        jnp.concatenate([mixed_mine, mixed_other], axis=1),
        jnp.concatenate([mixed_other, mixed_mine], axis=1),
    )


def solution(mesh):
    placed = (
        P(("req", "tp"), None),
        P(None, "tp"),
        P(None, None, "tp"),
        P("tp", None),
        P("req", "tp"),
        P("req", "tp"),
        P(),
        P(),
        P(),
        P("req"),
    )
    return jax.shard_map(
        per_device, mesh=mesh, in_specs=placed, out_specs=P(("req", "tp"), None), check_vma=False
    )
```

```python
import jax
import jax.numpy as jnp
from jax import lax
from jax.sharding import PartitionSpec as P
from jax.experimental import pallas as pl
from jax.experimental.pallas import tpu as pltpu

HEAD_DIM = 128
GROUP = 1024
MOST = 3


ROTARY_BASE = 10000.0
EPSILON = 1e-05
MASKED = -1e30


def from_behind(x, axis, by):
    length = lax.axis_size(axis)
    pairs = [(i, i + by) for i in range(length) if 0 <= i + by < length]
    return lax.ppermute(x, axis, pairs)


def frequencies(half_dim):
    indices = jnp.arange(half_dim, dtype=jnp.float32)
    return jnp.exp(indices * (-jnp.log(jnp.float32(ROTARY_BASE)) / half_dim))


def rotation_tables(angles, width):
    cosine = jnp.cos(angles)
    sine_part = jnp.sin(angles)
    repeats = width // (2 * angles.shape[-1])
    cos_full = jnp.tile(jnp.concatenate([cosine, cosine], axis=-1), (1, repeats))
    sin_full = jnp.tile(jnp.concatenate([-sine_part, sine_part], axis=-1), (1, repeats))
    return cos_full, sin_full


def rotate_flat(vectors, cos_full, sin_full):
    half_dim = HEAD_DIM // 2
    width = vectors.shape[-1]
    column = jnp.arange(width, dtype=jnp.int32) % HEAD_DIM
    partner = jnp.where(
        (column < half_dim)[None, :],
        jnp.roll(vectors, -half_dim, axis=1),
        jnp.roll(vectors, half_dim, axis=1),
    )
    return vectors * cos_full + partner * sin_full


def group_layout(request_lengths, group_order):
    group_count = group_order.shape[0]
    request_ends = jnp.cumsum(request_lengths)
    group_ids = jnp.arange(group_count, dtype=jnp.int32)
    group_request = jnp.sum((group_ids[:, None] >= request_ends[None, :]).astype(jnp.int32), axis=1)
    same_request = group_request[:, None] == group_request[None, :]
    earlier = group_order[None, :] < group_order[:, None]
    group_rank = jnp.sum((same_request & earlier).astype(jnp.int32), axis=1)
    return (group_request, group_rank)


def layer_norm(rows_in):
    values32 = rows_in.astype(jnp.float32)
    row_mean = jnp.mean(values32, axis=1, keepdims=True)
    centered = values32 - row_mean
    variance = jnp.mean(centered * centered, axis=1, keepdims=True)
    return (centered * lax.rsqrt(variance + EPSILON)).astype(jnp.bfloat16)


def attend(queries, joined_keys, joined_values, visible):
    row_count = queries.shape[0]
    key_count = joined_keys.shape[0]
    head_count = queries.shape[1] // HEAD_DIM
    query_heads = queries.reshape(row_count, head_count, HEAD_DIM)
    key_heads = joined_keys.reshape(key_count, head_count, HEAD_DIM)
    value_heads = joined_values.reshape(key_count, head_count, HEAD_DIM)
    scores = jnp.einsum(
        "qhd,khd->hqk", query_heads, key_heads, preferred_element_type=jnp.float32
    ) * HEAD_DIM ** (-0.5)
    if visible is not None:
        scores = jnp.where(visible[None], scores, MASKED)
    row_max = jnp.max(scores, axis=2)
    weights = jnp.exp(scores - row_max[:, :, None])
    if visible is not None:
        weights = jnp.where(visible[None], weights, 0.0)
    denominator = jnp.sum(weights, axis=2)
    numerator = jnp.einsum(
        "hqk,khd->qhd",
        weights.astype(jnp.bfloat16),
        value_heads,
        preferred_element_type=jnp.float32,
    )
    return (numerator, row_max, denominator)


def combine(first, second):
    row_max = jnp.maximum(first[1], second[1])
    scale_first = jnp.exp(first[1] - row_max)
    scale_second = jnp.exp(second[1] - row_max)
    numerator = (
        first[0] * jnp.transpose(scale_first)[:, :, None]
        + second[0] * jnp.transpose(scale_second)[:, :, None]
    )
    denominator = first[2] * scale_first + second[2] * scale_second
    return (numerator, row_max, denominator)


def attention_kernel(flags_ref, index_ref, query_ref, own_key_ref, own_value_ref, *refs):
    far_refs = refs[:-1]
    out_ref = refs[-1]
    scale = HEAD_DIM ** (-0.5)
    query = query_ref[...]
    scores = (
        lax.dot_general(
            query, own_key_ref[...], (((1,), (1,)), ((), ())), preferred_element_type=jnp.float32
        )
        * scale
    )
    key_ids = lax.broadcasted_iota(jnp.int32, scores.shape, 1)
    visible = key_ids <= index_ref[...]
    scores = jnp.where(visible, scores, MASKED)
    row_max = jnp.max(scores, axis=1, keepdims=True)
    weights = jnp.where(visible, jnp.exp(scores - row_max), 0.0)
    state = (
        row_max,
        jnp.sum(weights, axis=1, keepdims=True),
        jnp.dot(weights.astype(jnp.bfloat16), own_value_ref[...], preferred_element_type=jnp.float32),
    )
    slot_count = len(far_refs) // 4
    for slot in range(slot_count):
        kept_key, kept_value, fresh_key, fresh_value = far_refs[4 * slot : 4 * slot + 4]

        def block(key_ref, value_ref, carry):
            old_max, old_sum, old_acc = carry
            block_scores = (
                lax.dot_general(
                    query, key_ref[...], (((1,), (1,)), ((), ())),
                    preferred_element_type=jnp.float32,
                )
                * scale
            )
            new_max = jnp.maximum(old_max, jnp.max(block_scores, axis=1, keepdims=True))
            keep = jnp.exp(old_max - new_max)
            block_weights = jnp.exp(block_scores - new_max)
            return (
                new_max,
                keep * old_sum + jnp.sum(block_weights, axis=1, keepdims=True),
                keep * old_acc
                + jnp.dot(
                    block_weights.astype(jnp.bfloat16), value_ref[...],
                    preferred_element_type=jnp.float32,
                ),
            )

        def both(carry, kept_key=kept_key, kept_value=kept_value,
                 fresh_key=fresh_key, fresh_value=fresh_value):
            return block(fresh_key, fresh_value, block(kept_key, kept_value, carry))

        state = lax.cond(flags_ref[slot] != 0, both, lambda carry: carry, state)
    out_ref[...] = (state[2] / state[1]).astype(out_ref.dtype)


def fused_attention(flags, recompute_index, queries, joined_kv, far_parts):
    row_count, feature_width = queries.shape
    head_count = feature_width // HEAD_DIM
    key_count = joined_kv.shape[0]

    def column_spec(rows, offset, slot=None):
        if slot is None:
            return pl.BlockSpec((rows, HEAD_DIM), lambda h, flags_ref: (0, h + offset))
        return pl.BlockSpec(
            (rows, HEAD_DIM), lambda h, flags_ref: (0, (h + offset) * flags_ref[slot])
        )

    in_specs = [
        pl.BlockSpec((row_count, 1), lambda h, flags_ref: (0, 0)),
        column_spec(row_count, 0),
        column_spec(key_count, 0),
        column_spec(key_count, head_count),
    ]
    operands = [recompute_index.reshape(row_count, 1), queries, joined_kv, joined_kv]
    for slot, (kept_part, fresh_part) in enumerate(far_parts):
        in_specs += [
            column_spec(kept_part.shape[0], 0, slot),
            column_spec(kept_part.shape[0], head_count, slot),
            column_spec(fresh_part.shape[0], 0, slot),
            column_spec(fresh_part.shape[0], head_count, slot),
        ]
        operands += [kept_part, kept_part, fresh_part, fresh_part]
    grid_spec = pltpu.PrefetchScalarGridSpec(
        num_scalar_prefetch=1,
        grid=(head_count,),
        in_specs=in_specs,
        out_specs=pl.BlockSpec((row_count, HEAD_DIM), lambda h, flags_ref: (0, h)),
    )
    return pl.pallas_call(
        attention_kernel,
        grid_spec=grid_spec,
        out_shape=jax.ShapeDtypeStruct((row_count, feature_width), jnp.bfloat16),
        compiler_params=pltpu.CompilerParams(vmem_limit_bytes=48 * 1024 * 1024),
    )(flags, *operands)


def per_device(
    tokens,
    query_weight,
    kv_weight,
    out_weight,
    cached_keys,
    cached_values,
    request_lengths,
    group_order,
    group_offset,
    recompute_index,
):
    feature_width = query_weight.shape[1]
    head_count = feature_width // HEAD_DIM
    half_dim = HEAD_DIM // 2
    group_count = group_order.shape[0]
    tp_size = lax.axis_size("tp")
    device = lax.axis_index("req")
    tp_index = lax.axis_index("tp")
    group_request, group_rank = group_layout(request_lengths, group_order)
    own_request = group_request[device]
    own_rank = group_rank[device]
    core = device % 2
    half_width = out_weight.shape[1] // 2
    mine_half = lax.all_gather(
        lax.dynamic_slice_in_dim(out_weight, core * half_width, half_width, 1), "tp", axis=0, tiled=True
    )
    req_size = lax.axis_size("req")
    sibling = [(i, i ^ 1) for i in range(req_size)]
    freq = frequencies(half_dim)
    key_count = cached_keys.shape[0]
    row_count = recompute_index.shape[0]

    rotation = (own_rank * GROUP - group_offset[device]).astype(jnp.float32)
    group_cos, group_sin = rotation_tables((rotation * freq)[None, :], feature_width)
    rotated_keys = rotate_flat(cached_keys.astype(jnp.float32), group_cos, group_sin).astype(
        jnp.bfloat16
    )
    cached_kv = jnp.concatenate([rotated_keys, cached_values], axis=1)

    key_ids = jnp.arange(key_count, dtype=jnp.int32)
    placement = key_ids[:, None] == recompute_index[None, :]
    replaced = jnp.any(placement, axis=1)
    replaced_before = jnp.sum((recompute_index[None, :] < key_ids[:, None]).astype(jnp.int32), axis=1)
    kept_slot = key_ids - replaced_before
    packing = (~replaced)[None, :] & (
        jnp.arange(key_count - row_count, dtype=jnp.int32)[:, None] == kept_slot[None, :]
    )
    kept_kv = jnp.dot(
        packing.astype(jnp.bfloat16), cached_kv, preferred_element_type=jnp.float32
    ).astype(jnp.bfloat16)

    distances = [distance for distance in range(1, MOST)] + [
        -distance for distance in range(1, MOST)
    ]
    far_kept = [from_behind(kept_kv, "req", distance) for distance in distances]

    local_rows = layer_norm(tokens)
    row_pieces = [local_rows]
    for shift in range(1, tp_size):
        pairs = [(peer, (peer + shift) % tp_size) for peer in range(tp_size)]
        row_pieces.append(lax.ppermute(local_rows, "tp", pairs))
    row_stack = jnp.stack(row_pieces)
    normalized = jnp.concatenate(
        [row_stack[(tp_index - peer) % tp_size] for peer in range(tp_size)], axis=0
    )
    query_part = jnp.dot(normalized, query_weight, preferred_element_type=jnp.float32)
    kv_part = jnp.einsum("nd,dkc->knc", normalized, kv_weight, preferred_element_type=jnp.float32)
    key_part = kv_part[0]
    value_part = kv_part[1]
    positions = (own_rank * GROUP + recompute_index).astype(jnp.float32)
    row_cos, row_sin = rotation_tables(positions[:, None] * freq[None, :], feature_width)
    queries = rotate_flat(query_part, row_cos, row_sin).astype(jnp.bfloat16)
    fresh_keys = rotate_flat(key_part, row_cos, row_sin).astype(jnp.bfloat16)
    fresh_values = value_part.astype(jnp.bfloat16)
    fresh_kv = jnp.concatenate([fresh_keys, fresh_values], axis=1)
    far_fresh = [from_behind(fresh_kv, "req", distance) for distance in distances]

    placed_kv = jnp.dot(
        placement.astype(jnp.bfloat16), fresh_kv, preferred_element_type=jnp.float32
    ).astype(jnp.bfloat16)
    joined_kv = jnp.where(replaced[:, None], placed_kv, cached_kv)
    flags = []
    for distance in distances:
        source_index = jnp.clip(device - distance, 0, group_count - 1)
        source_inside = (device - distance >= 0) & (device - distance < group_count)
        needed = (
            source_inside
            & (group_request[source_index] == own_request)
            & (group_rank[source_index] < own_rank)
        )
        flags.append(needed.astype(jnp.int32))
    attention = fused_attention(
        jnp.stack(flags), recompute_index, queries, joined_kv, list(zip(far_kept, far_fresh))
    )

    chunk = row_count // tp_size

    def rows_for(peer):
        return lax.dynamic_slice_in_dim(attention, peer * chunk, chunk, 0)

    pieces = [rows_for(tp_index)]
    for shift in range(1, tp_size):
        pairs = [(peer, (peer + shift) % tp_size) for peer in range(tp_size)]
        pieces.append(lax.ppermute(rows_for((tp_index + shift) % tp_size), "tp", pairs))
    arrived = jnp.stack(pieces)
    own_rows = jnp.concatenate(
        [arrived[(tp_index - peer) % tp_size] for peer in range(tp_size)], axis=1
    )
    sibling_rows = lax.ppermute(own_rows, "req", sibling)
    both_rows = jnp.concatenate([own_rows, sibling_rows], axis=0)
    both_mixed = jnp.dot(both_rows, mine_half, preferred_element_type=jnp.float32).astype(jnp.bfloat16)
    chunk_rows = own_rows.shape[0]
    mixed_mine = both_mixed[:chunk_rows]
    mixed_other = lax.ppermute(both_mixed[chunk_rows:], "req", sibling)
    return jnp.where(
        core == 0,
        jnp.concatenate([mixed_mine, mixed_other], axis=1),
        jnp.concatenate([mixed_other, mixed_mine], axis=1),
    )


def solution(mesh):
    placed = (
        P(("req", "tp"), None),
        P(None, "tp"),
        P(None, None, "tp"),
        P("tp", None),
        P("req", "tp"),
        P("req", "tp"),
        P(),
        P(),
        P(),
        P("req"),
    )
    return jax.shard_map(
        per_device, mesh=mesh, in_specs=placed, out_specs=P(("req", "tp"), None), check_vma=False
    )
```

```python
import jax
import jax.numpy as jnp
from jax import lax
from jax.sharding import PartitionSpec as P
from jax.experimental import pallas as pl
from jax.experimental.pallas import tpu as pltpu

HEAD_DIM = 128
GROUP = 1024
MOST = 3


ROTARY_BASE = 10000.0
EPSILON = 1e-05
MASKED = -1e30


def from_behind(x, axis, by):
    length = lax.axis_size(axis)
    pairs = [(i, i + by) for i in range(length) if 0 <= i + by < length]
    return lax.ppermute(x, axis, pairs)


def frequencies(half_dim):
    indices = jnp.arange(half_dim, dtype=jnp.float32)
    return jnp.exp(indices * (-jnp.log(jnp.float32(ROTARY_BASE)) / half_dim))


def rotation_tables(angles, width):
    cosine = jnp.cos(angles)
    sine_part = jnp.sin(angles)
    repeats = width // (2 * angles.shape[-1])
    cos_full = jnp.tile(jnp.concatenate([cosine, cosine], axis=-1), (1, repeats))
    sin_full = jnp.tile(jnp.concatenate([-sine_part, sine_part], axis=-1), (1, repeats))
    return cos_full, sin_full


def rotate_flat(vectors, cos_full, sin_full):
    half_dim = HEAD_DIM // 2
    width = vectors.shape[-1]
    column = jnp.arange(width, dtype=jnp.int32) % HEAD_DIM
    partner = jnp.where(
        (column < half_dim)[None, :],
        jnp.roll(vectors, -half_dim, axis=1),
        jnp.roll(vectors, half_dim, axis=1),
    )
    return vectors * cos_full + partner * sin_full


def group_layout(request_lengths, group_order):
    group_count = group_order.shape[0]
    request_ends = jnp.cumsum(request_lengths)
    group_ids = jnp.arange(group_count, dtype=jnp.int32)
    group_request = jnp.sum((group_ids[:, None] >= request_ends[None, :]).astype(jnp.int32), axis=1)
    same_request = group_request[:, None] == group_request[None, :]
    earlier = group_order[None, :] < group_order[:, None]
    group_rank = jnp.sum((same_request & earlier).astype(jnp.int32), axis=1)
    return (group_request, group_rank)


def layer_norm(rows_in):
    values32 = rows_in.astype(jnp.float32)
    row_mean = jnp.mean(values32, axis=1, keepdims=True)
    centered = values32 - row_mean
    variance = jnp.mean(centered * centered, axis=1, keepdims=True)
    return (centered * lax.rsqrt(variance + EPSILON)).astype(jnp.bfloat16)


def attend(queries, joined_keys, joined_values, visible):
    row_count = queries.shape[0]
    key_count = joined_keys.shape[0]
    head_count = queries.shape[1] // HEAD_DIM
    query_heads = queries.reshape(row_count, head_count, HEAD_DIM)
    key_heads = joined_keys.reshape(key_count, head_count, HEAD_DIM)
    value_heads = joined_values.reshape(key_count, head_count, HEAD_DIM)
    scores = jnp.einsum(
        "qhd,khd->hqk", query_heads, key_heads, preferred_element_type=jnp.float32
    ) * HEAD_DIM ** (-0.5)
    if visible is not None:
        scores = jnp.where(visible[None], scores, MASKED)
    row_max = jnp.max(scores, axis=2)
    weights = jnp.exp(scores - row_max[:, :, None])
    if visible is not None:
        weights = jnp.where(visible[None], weights, 0.0)
    denominator = jnp.sum(weights, axis=2)
    numerator = jnp.einsum(
        "hqk,khd->qhd",
        weights.astype(jnp.bfloat16),
        value_heads,
        preferred_element_type=jnp.float32,
    )
    return (numerator, row_max, denominator)


def combine(first, second):
    row_max = jnp.maximum(first[1], second[1])
    scale_first = jnp.exp(first[1] - row_max)
    scale_second = jnp.exp(second[1] - row_max)
    numerator = (
        first[0] * jnp.transpose(scale_first)[:, :, None]
        + second[0] * jnp.transpose(scale_second)[:, :, None]
    )
    denominator = first[2] * scale_first + second[2] * scale_second
    return (numerator, row_max, denominator)


def own_attention_kernel(index_ref, query_ref, own_key_ref, own_value_ref, max_ref, sum_ref, acc_ref):
    scale = HEAD_DIM ** (-0.5)
    scores = (
        lax.dot_general(
            query_ref[...], own_key_ref[...], (((1,), (1,)), ((), ())),
            preferred_element_type=jnp.float32,
        )
        * scale
    )
    key_ids = lax.broadcasted_iota(jnp.int32, scores.shape, 1)
    visible = key_ids <= index_ref[...]
    scores = jnp.where(visible, scores, MASKED)
    row_max = jnp.max(scores, axis=1, keepdims=True)
    weights = jnp.where(visible, jnp.exp(scores - row_max), 0.0)
    max_ref[...] = jnp.broadcast_to(row_max, max_ref.shape)
    sum_ref[...] = jnp.broadcast_to(jnp.sum(weights, axis=1, keepdims=True), sum_ref.shape)
    acc_ref[...] = jnp.dot(
        weights.astype(jnp.bfloat16), own_value_ref[...], preferred_element_type=jnp.float32
    )


def far_attention_kernel(flags_ref, query_ref, max_ref, sum_ref, acc_ref, *refs):
    far_refs = refs[:-1]
    out_ref = refs[-1]
    scale = HEAD_DIM ** (-0.5)
    query = query_ref[...]
    state = (max_ref[:, :1], sum_ref[:, :1], acc_ref[...])
    slot_count = len(far_refs) // 4
    for slot in range(slot_count):
        kept_key, kept_value, fresh_key, fresh_value = far_refs[4 * slot : 4 * slot + 4]

        def block(key_ref, value_ref, carry):
            old_max, old_sum, old_acc = carry
            block_scores = (
                lax.dot_general(
                    query, key_ref[...], (((1,), (1,)), ((), ())),
                    preferred_element_type=jnp.float32,
                )
                * scale
            )
            new_max = jnp.maximum(old_max, jnp.max(block_scores, axis=1, keepdims=True))
            keep = jnp.exp(old_max - new_max)
            block_weights = jnp.exp(block_scores - new_max)
            return (
                new_max,
                keep * old_sum + jnp.sum(block_weights, axis=1, keepdims=True),
                keep * old_acc
                + jnp.dot(
                    block_weights.astype(jnp.bfloat16), value_ref[...],
                    preferred_element_type=jnp.float32,
                ),
            )

        def both(carry, kept_key=kept_key, kept_value=kept_value,
                 fresh_key=fresh_key, fresh_value=fresh_value):
            return block(fresh_key, fresh_value, block(kept_key, kept_value, carry))

        state = lax.cond(flags_ref[slot] != 0, both, lambda carry: carry, state)
    out_ref[...] = (state[2] / state[1]).astype(out_ref.dtype)


def fused_attention(flags, recompute_index, queries, joined_kv, far_parts):
    row_count, feature_width = queries.shape
    head_count = feature_width // HEAD_DIM
    key_count = joined_kv.shape[0]
    params = pltpu.CompilerParams(vmem_limit_bytes=48 * 1024 * 1024)
    head_block = pl.BlockSpec((row_count, HEAD_DIM), lambda h: (0, h))
    state_shape = jax.ShapeDtypeStruct((row_count, feature_width), jnp.float32)
    running = pl.pallas_call(
        own_attention_kernel,
        grid=(head_count,),
        in_specs=[
            pl.BlockSpec((row_count, 1), lambda h: (0, 0)),
            head_block,
            pl.BlockSpec((key_count, HEAD_DIM), lambda h: (0, h)),
            pl.BlockSpec((key_count, HEAD_DIM), lambda h: (0, h + head_count)),
        ],
        out_specs=[head_block, head_block, head_block],
        out_shape=[state_shape, state_shape, state_shape],
        compiler_params=params,
    )(recompute_index.reshape(row_count, 1), queries, joined_kv, joined_kv)

    def column_spec(rows, offset, slot=None):
        if slot is None:
            return pl.BlockSpec((rows, HEAD_DIM), lambda h, flags_ref: (0, h + offset))
        return pl.BlockSpec(
            (rows, HEAD_DIM), lambda h, flags_ref: (0, (h + offset) * flags_ref[slot])
        )

    in_specs = [column_spec(row_count, 0)] * 4
    operands = [queries, *running]
    for slot, (kept_part, fresh_part) in enumerate(far_parts):
        in_specs += [
            column_spec(kept_part.shape[0], 0, slot),
            column_spec(kept_part.shape[0], head_count, slot),
            column_spec(fresh_part.shape[0], 0, slot),
            column_spec(fresh_part.shape[0], head_count, slot),
        ]
        operands += [kept_part, kept_part, fresh_part, fresh_part]
    grid_spec = pltpu.PrefetchScalarGridSpec(
        num_scalar_prefetch=1,
        grid=(head_count,),
        in_specs=in_specs,
        out_specs=column_spec(row_count, 0),
    )
    return pl.pallas_call(
        far_attention_kernel,
        grid_spec=grid_spec,
        out_shape=jax.ShapeDtypeStruct((row_count, feature_width), jnp.bfloat16),
        compiler_params=params,
    )(flags, *operands)


def per_device(
    tokens,
    query_weight,
    kv_weight,
    out_weight,
    cached_keys,
    cached_values,
    request_lengths,
    group_order,
    group_offset,
    recompute_index,
):
    feature_width = query_weight.shape[1]
    head_count = feature_width // HEAD_DIM
    half_dim = HEAD_DIM // 2
    group_count = group_order.shape[0]
    tp_size = lax.axis_size("tp")
    device = lax.axis_index("req")
    tp_index = lax.axis_index("tp")
    group_request, group_rank = group_layout(request_lengths, group_order)
    own_request = group_request[device]
    own_rank = group_rank[device]
    core = device % 2
    half_width = out_weight.shape[1] // 2
    mine_half = lax.all_gather(
        lax.dynamic_slice_in_dim(out_weight, core * half_width, half_width, 1), "tp", axis=0, tiled=True
    )
    req_size = lax.axis_size("req")
    sibling = [(i, i ^ 1) for i in range(req_size)]
    freq = frequencies(half_dim)
    key_count = cached_keys.shape[0]
    row_count = recompute_index.shape[0]

    rotation = (own_rank * GROUP - group_offset[device]).astype(jnp.float32)
    group_cos, group_sin = rotation_tables((rotation * freq)[None, :], feature_width)
    rotated_keys = rotate_flat(cached_keys.astype(jnp.float32), group_cos, group_sin).astype(
        jnp.bfloat16
    )
    cached_kv = jnp.concatenate([rotated_keys, cached_values], axis=1)

    key_ids = jnp.arange(key_count, dtype=jnp.int32)
    placement = key_ids[:, None] == recompute_index[None, :]
    replaced = jnp.any(placement, axis=1)
    replaced_before = jnp.sum((recompute_index[None, :] < key_ids[:, None]).astype(jnp.int32), axis=1)
    kept_slot = key_ids - replaced_before
    packing = (~replaced)[None, :] & (
        jnp.arange(key_count - row_count, dtype=jnp.int32)[:, None] == kept_slot[None, :]
    )
    kept_kv = jnp.dot(
        packing.astype(jnp.bfloat16), cached_kv, preferred_element_type=jnp.float32
    ).astype(jnp.bfloat16)

    distances = [distance for distance in range(1, MOST)] + [
        -distance for distance in range(1, MOST)
    ]
    far_kept = [from_behind(kept_kv, "req", distance) for distance in distances]

    local_rows = layer_norm(tokens)
    row_pieces = [local_rows]
    for shift in range(1, tp_size):
        pairs = [(peer, (peer + shift) % tp_size) for peer in range(tp_size)]
        row_pieces.append(lax.ppermute(local_rows, "tp", pairs))
    row_stack = jnp.stack(row_pieces)
    normalized = jnp.concatenate(
        [row_stack[(tp_index - peer) % tp_size] for peer in range(tp_size)], axis=0
    )
    query_part = jnp.dot(normalized, query_weight, preferred_element_type=jnp.float32)
    kv_part = jnp.einsum("nd,dkc->knc", normalized, kv_weight, preferred_element_type=jnp.float32)
    key_part = kv_part[0]
    value_part = kv_part[1]
    positions = (own_rank * GROUP + recompute_index).astype(jnp.float32)
    row_cos, row_sin = rotation_tables(positions[:, None] * freq[None, :], feature_width)
    queries = rotate_flat(query_part, row_cos, row_sin).astype(jnp.bfloat16)
    fresh_keys = rotate_flat(key_part, row_cos, row_sin).astype(jnp.bfloat16)
    fresh_values = value_part.astype(jnp.bfloat16)
    fresh_kv = jnp.concatenate([fresh_keys, fresh_values], axis=1)
    far_fresh = [from_behind(fresh_kv, "req", distance) for distance in distances]

    placed_kv = jnp.dot(
        placement.astype(jnp.bfloat16), fresh_kv, preferred_element_type=jnp.float32
    ).astype(jnp.bfloat16)
    joined_kv = jnp.where(replaced[:, None], placed_kv, cached_kv)
    flags = []
    for distance in distances:
        source_index = jnp.clip(device - distance, 0, group_count - 1)
        source_inside = (device - distance >= 0) & (device - distance < group_count)
        needed = (
            source_inside
            & (group_request[source_index] == own_request)
            & (group_rank[source_index] < own_rank)
        )
        flags.append(needed.astype(jnp.int32))
    attention = fused_attention(
        jnp.stack(flags), recompute_index, queries, joined_kv, list(zip(far_kept, far_fresh))
    )

    chunk = row_count // tp_size

    def rows_for(peer):
        return lax.dynamic_slice_in_dim(attention, peer * chunk, chunk, 0)

    pieces = [rows_for(tp_index)]
    for shift in range(1, tp_size):
        pairs = [(peer, (peer + shift) % tp_size) for peer in range(tp_size)]
        pieces.append(lax.ppermute(rows_for((tp_index + shift) % tp_size), "tp", pairs))
    arrived = jnp.stack(pieces)
    own_rows = jnp.concatenate(
        [arrived[(tp_index - peer) % tp_size] for peer in range(tp_size)], axis=1
    )
    sibling_rows = lax.ppermute(own_rows, "req", sibling)
    both_rows = jnp.concatenate([own_rows, sibling_rows], axis=0)
    both_mixed = jnp.dot(both_rows, mine_half, preferred_element_type=jnp.float32).astype(jnp.bfloat16)
    chunk_rows = own_rows.shape[0]
    mixed_mine = both_mixed[:chunk_rows]
    mixed_other = lax.ppermute(both_mixed[chunk_rows:], "req", sibling)
    return jnp.where(
        core == 0,
        jnp.concatenate([mixed_mine, mixed_other], axis=1),
        jnp.concatenate([mixed_other, mixed_mine], axis=1),
    )


def solution(mesh):
    placed = (
        P(("req", "tp"), None),
        P(None, "tp"),
        P(None, None, "tp"),
        P("tp", None),
        P("req", "tp"),
        P("req", "tp"),
        P(),
        P(),
        P(),
        P("req"),
    )
    return jax.shard_map(
        per_device, mesh=mesh, in_specs=placed, out_specs=P(("req", "tp"), None), check_vma=False
    )
```

```python
import functools

import jax
import jax.numpy as jnp
from jax import lax
from jax.sharding import PartitionSpec as P
from jax.experimental import pallas as pl
from jax.experimental.pallas import tpu as pltpu

HEAD_DIM = 128
GROUP = 1024
MOST = 3


ROTARY_BASE = 10000.0
EPSILON = 1e-05
MASKED = -1e30


def from_behind(x, axis, by):
    length = lax.axis_size(axis)
    pairs = [(i, i + by) for i in range(length) if 0 <= i + by < length]
    return lax.ppermute(x, axis, pairs)


def frequencies(half_dim):
    indices = jnp.arange(half_dim, dtype=jnp.float32)
    return jnp.exp(indices * (-jnp.log(jnp.float32(ROTARY_BASE)) / half_dim))


def rotation_tables(angles, width):
    cosine = jnp.cos(angles)
    sine_part = jnp.sin(angles)
    repeats = width // (2 * angles.shape[-1])
    cos_full = jnp.tile(jnp.concatenate([cosine, cosine], axis=-1), (1, repeats))
    sin_full = jnp.tile(jnp.concatenate([-sine_part, sine_part], axis=-1), (1, repeats))
    return cos_full, sin_full


def rotate_flat(vectors, cos_full, sin_full):
    half_dim = HEAD_DIM // 2
    width = vectors.shape[-1]
    column = jnp.arange(width, dtype=jnp.int32) % HEAD_DIM
    partner = jnp.where(
        (column < half_dim)[None, :],
        jnp.roll(vectors, -half_dim, axis=1),
        jnp.roll(vectors, half_dim, axis=1),
    )
    return vectors * cos_full + partner * sin_full


def group_layout(request_lengths, group_order):
    group_count = group_order.shape[0]
    request_ends = jnp.cumsum(request_lengths)
    group_ids = jnp.arange(group_count, dtype=jnp.int32)
    group_request = jnp.sum((group_ids[:, None] >= request_ends[None, :]).astype(jnp.int32), axis=1)
    same_request = group_request[:, None] == group_request[None, :]
    earlier = group_order[None, :] < group_order[:, None]
    group_rank = jnp.sum((same_request & earlier).astype(jnp.int32), axis=1)
    return (group_request, group_rank)


def layer_norm(rows_in):
    values32 = rows_in.astype(jnp.float32)
    row_mean = jnp.mean(values32, axis=1, keepdims=True)
    centered = values32 - row_mean
    variance = jnp.mean(centered * centered, axis=1, keepdims=True)
    return (centered * lax.rsqrt(variance + EPSILON)).astype(jnp.bfloat16)


def attend(queries, joined_keys, joined_values, visible):
    row_count = queries.shape[0]
    key_count = joined_keys.shape[0]
    head_count = queries.shape[1] // HEAD_DIM
    query_heads = queries.reshape(row_count, head_count, HEAD_DIM)
    key_heads = joined_keys.reshape(key_count, head_count, HEAD_DIM)
    value_heads = joined_values.reshape(key_count, head_count, HEAD_DIM)
    scores = jnp.einsum(
        "qhd,khd->hqk", query_heads, key_heads, preferred_element_type=jnp.float32
    ) * HEAD_DIM ** (-0.5)
    if visible is not None:
        scores = jnp.where(visible[None], scores, MASKED)
    row_max = jnp.max(scores, axis=2)
    weights = jnp.exp(scores - row_max[:, :, None])
    if visible is not None:
        weights = jnp.where(visible[None], weights, 0.0)
    denominator = jnp.sum(weights, axis=2)
    numerator = jnp.einsum(
        "hqk,khd->qhd",
        weights.astype(jnp.bfloat16),
        value_heads,
        preferred_element_type=jnp.float32,
    )
    return (numerator, row_max, denominator)


def combine(first, second):
    row_max = jnp.maximum(first[1], second[1])
    scale_first = jnp.exp(first[1] - row_max)
    scale_second = jnp.exp(second[1] - row_max)
    numerator = (
        first[0] * jnp.transpose(scale_first)[:, :, None]
        + second[0] * jnp.transpose(scale_second)[:, :, None]
    )
    denominator = first[2] * scale_first + second[2] * scale_second
    return (numerator, row_max, denominator)


def own_attention_kernel(index_ref, query_ref, own_key_ref, own_value_ref, max_ref, sum_ref, acc_ref):
    scale = HEAD_DIM ** (-0.5)
    scores = (
        lax.dot_general(
            query_ref[...], own_key_ref[...], (((1,), (1,)), ((), ())),
            preferred_element_type=jnp.float32,
        )
        * scale
    )
    key_ids = lax.broadcasted_iota(jnp.int32, scores.shape, 1)
    visible = key_ids <= index_ref[...]
    scores = jnp.where(visible, scores, MASKED)
    row_max = jnp.max(scores, axis=1, keepdims=True)
    weights = jnp.where(visible, jnp.exp(scores - row_max), 0.0)
    max_ref[...] = jnp.broadcast_to(row_max, max_ref.shape)
    sum_ref[...] = jnp.broadcast_to(jnp.sum(weights, axis=1, keepdims=True), sum_ref.shape)
    acc_ref[...] = jnp.dot(
        weights.astype(jnp.bfloat16), own_value_ref[...], preferred_element_type=jnp.float32
    )


def far_attention_kernel(final, flags_ref, query_ref, max_ref, sum_ref, acc_ref, *refs):
    output_count = 1 if final else 3
    far_refs = refs[:-output_count]
    out_refs = refs[-output_count:]
    scale = HEAD_DIM ** (-0.5)
    query = query_ref[...]
    state = (max_ref[:, :1], sum_ref[:, :1], acc_ref[...])
    for slot in range(len(far_refs) // 2):
        key_ref, value_ref = far_refs[2 * slot : 2 * slot + 2]

        def block(carry, key_ref=key_ref, value_ref=value_ref):
            old_max, old_sum, old_acc = carry
            block_scores = (
                lax.dot_general(
                    query, key_ref[...], (((1,), (1,)), ((), ())),
                    preferred_element_type=jnp.float32,
                )
                * scale
            )
            new_max = jnp.maximum(old_max, jnp.max(block_scores, axis=1, keepdims=True))
            keep = jnp.exp(old_max - new_max)
            block_weights = jnp.exp(block_scores - new_max)
            return (
                new_max,
                keep * old_sum + jnp.sum(block_weights, axis=1, keepdims=True),
                keep * old_acc
                + jnp.dot(
                    block_weights.astype(jnp.bfloat16), value_ref[...],
                    preferred_element_type=jnp.float32,
                ),
            )

        state = lax.cond(flags_ref[slot] != 0, block, lambda carry: carry, state)
    if final:
        out_refs[0][...] = (state[2] / state[1]).astype(out_refs[0].dtype)
    else:
        out_refs[0][...] = jnp.broadcast_to(state[0], out_refs[0].shape)
        out_refs[1][...] = jnp.broadcast_to(state[1], out_refs[1].shape)
        out_refs[2][...] = state[2]


def fused_attention(flags, recompute_index, queries, joined_kv, far_parts):
    row_count, feature_width = queries.shape
    head_count = feature_width // HEAD_DIM
    key_count = joined_kv.shape[0]
    params = pltpu.CompilerParams(vmem_limit_bytes=48 * 1024 * 1024)
    head_block = pl.BlockSpec((row_count, HEAD_DIM), lambda h: (0, h))
    state_shape = jax.ShapeDtypeStruct((row_count, feature_width), jnp.float32)
    running = pl.pallas_call(
        own_attention_kernel,
        grid=(head_count,),
        in_specs=[
            pl.BlockSpec((row_count, 1), lambda h: (0, 0)),
            head_block,
            pl.BlockSpec((key_count, HEAD_DIM), lambda h: (0, h)),
            pl.BlockSpec((key_count, HEAD_DIM), lambda h: (0, h + head_count)),
        ],
        out_specs=[head_block, head_block, head_block],
        out_shape=[state_shape, state_shape, state_shape],
        compiler_params=params,
    )(recompute_index.reshape(row_count, 1), queries, joined_kv, joined_kv)

    def column_spec(rows, offset, slot=None):
        if slot is None:
            return pl.BlockSpec((rows, HEAD_DIM), lambda h, flags_ref: (0, h + offset))
        return pl.BlockSpec(
            (rows, HEAD_DIM), lambda h, flags_ref: (0, (h + offset) * flags_ref[slot])
        )

    for part_index, final in ((0, False), (1, True)):
        in_specs = [column_spec(row_count, 0)] * 4
        operands = [queries, *running]
        for slot, parts in enumerate(far_parts):
            part = parts[part_index]
            in_specs += [
                column_spec(part.shape[0], 0, slot),
                column_spec(part.shape[0], head_count, slot),
            ]
            operands += [part, part]
        out_spec = column_spec(row_count, 0)
        grid_spec = pltpu.PrefetchScalarGridSpec(
            num_scalar_prefetch=1,
            grid=(head_count,),
            in_specs=in_specs,
            out_specs=out_spec if final else [out_spec] * 3,
        )
        out_shape = (
            jax.ShapeDtypeStruct((row_count, feature_width), jnp.bfloat16)
            if final
            else [state_shape] * 3
        )
        running = pl.pallas_call(
            functools.partial(far_attention_kernel, final),
            grid_spec=grid_spec,
            out_shape=out_shape,
            compiler_params=params,
        )(flags, *operands)
    return running


def per_device(
    tokens,
    query_weight,
    kv_weight,
    out_weight,
    cached_keys,
    cached_values,
    request_lengths,
    group_order,
    group_offset,
    recompute_index,
):
    feature_width = query_weight.shape[1]
    head_count = feature_width // HEAD_DIM
    half_dim = HEAD_DIM // 2
    group_count = group_order.shape[0]
    tp_size = lax.axis_size("tp")
    device = lax.axis_index("req")
    tp_index = lax.axis_index("tp")
    group_request, group_rank = group_layout(request_lengths, group_order)
    own_request = group_request[device]
    own_rank = group_rank[device]
    core = device % 2
    half_width = out_weight.shape[1] // 2
    mine_half = lax.all_gather(
        lax.dynamic_slice_in_dim(out_weight, core * half_width, half_width, 1), "tp", axis=0, tiled=True
    )
    req_size = lax.axis_size("req")
    sibling = [(i, i ^ 1) for i in range(req_size)]
    freq = frequencies(half_dim)
    key_count = cached_keys.shape[0]
    row_count = recompute_index.shape[0]

    rotation = (own_rank * GROUP - group_offset[device]).astype(jnp.float32)
    group_cos, group_sin = rotation_tables((rotation * freq)[None, :], feature_width)
    rotated_keys = rotate_flat(cached_keys.astype(jnp.float32), group_cos, group_sin).astype(
        jnp.bfloat16
    )
    cached_kv = jnp.concatenate([rotated_keys, cached_values], axis=1)

    key_ids = jnp.arange(key_count, dtype=jnp.int32)
    placement = key_ids[:, None] == recompute_index[None, :]
    replaced = jnp.any(placement, axis=1)
    replaced_before = jnp.sum((recompute_index[None, :] < key_ids[:, None]).astype(jnp.int32), axis=1)
    kept_slot = key_ids - replaced_before
    packing = (~replaced)[None, :] & (
        jnp.arange(key_count - row_count, dtype=jnp.int32)[:, None] == kept_slot[None, :]
    )
    kept_kv = jnp.dot(
        packing.astype(jnp.bfloat16), cached_kv, preferred_element_type=jnp.float32
    ).astype(jnp.bfloat16)

    distances = [distance for distance in range(1, MOST)] + [
        -distance for distance in range(1, MOST)
    ]
    far_kept = [from_behind(kept_kv, "req", distance) for distance in distances]

    local_rows = layer_norm(tokens)
    row_pieces = [local_rows]
    for shift in range(1, tp_size):
        pairs = [(peer, (peer + shift) % tp_size) for peer in range(tp_size)]
        row_pieces.append(lax.ppermute(local_rows, "tp", pairs))
    row_stack = jnp.stack(row_pieces)
    normalized = jnp.concatenate(
        [row_stack[(tp_index - peer) % tp_size] for peer in range(tp_size)], axis=0
    )
    query_part = jnp.dot(normalized, query_weight, preferred_element_type=jnp.float32)
    kv_part = jnp.einsum("nd,dkc->knc", normalized, kv_weight, preferred_element_type=jnp.float32)
    key_part = kv_part[0]
    value_part = kv_part[1]
    positions = (own_rank * GROUP + recompute_index).astype(jnp.float32)
    row_cos, row_sin = rotation_tables(positions[:, None] * freq[None, :], feature_width)
    queries = rotate_flat(query_part, row_cos, row_sin).astype(jnp.bfloat16)
    fresh_keys = rotate_flat(key_part, row_cos, row_sin).astype(jnp.bfloat16)
    fresh_values = value_part.astype(jnp.bfloat16)
    fresh_kv = jnp.concatenate([fresh_keys, fresh_values], axis=1)
    far_fresh = [from_behind(fresh_kv, "req", distance) for distance in distances]

    placed_kv = jnp.dot(
        placement.astype(jnp.bfloat16), fresh_kv, preferred_element_type=jnp.float32
    ).astype(jnp.bfloat16)
    joined_kv = jnp.where(replaced[:, None], placed_kv, cached_kv)
    flags = []
    for distance in distances:
        source_index = jnp.clip(device - distance, 0, group_count - 1)
        source_inside = (device - distance >= 0) & (device - distance < group_count)
        needed = (
            source_inside
            & (group_request[source_index] == own_request)
            & (group_rank[source_index] < own_rank)
        )
        flags.append(needed.astype(jnp.int32))
    attention = fused_attention(
        jnp.stack(flags), recompute_index, queries, joined_kv, list(zip(far_kept, far_fresh))
    )

    chunk = row_count // tp_size

    def rows_for(peer):
        return lax.dynamic_slice_in_dim(attention, peer * chunk, chunk, 0)

    pieces = [rows_for(tp_index)]
    for shift in range(1, tp_size):
        pairs = [(peer, (peer + shift) % tp_size) for peer in range(tp_size)]
        pieces.append(lax.ppermute(rows_for((tp_index + shift) % tp_size), "tp", pairs))
    arrived = jnp.stack(pieces)
    own_rows = jnp.concatenate(
        [arrived[(tp_index - peer) % tp_size] for peer in range(tp_size)], axis=1
    )
    sibling_rows = lax.ppermute(own_rows, "req", sibling)
    both_rows = jnp.concatenate([own_rows, sibling_rows], axis=0)
    both_mixed = jnp.dot(both_rows, mine_half, preferred_element_type=jnp.float32).astype(jnp.bfloat16)
    chunk_rows = own_rows.shape[0]
    mixed_mine = both_mixed[:chunk_rows]
    mixed_other = lax.ppermute(both_mixed[chunk_rows:], "req", sibling)
    return jnp.where(
        core == 0,
        jnp.concatenate([mixed_mine, mixed_other], axis=1),
        jnp.concatenate([mixed_other, mixed_mine], axis=1),
    )


def solution(mesh):
    placed = (
        P(("req", "tp"), None),
        P(None, "tp"),
        P(None, None, "tp"),
        P("tp", None),
        P("req", "tp"),
        P("req", "tp"),
        P(),
        P(),
        P(),
        P("req"),
    )
    return jax.shard_map(
        per_device, mesh=mesh, in_specs=placed, out_specs=P(("req", "tp"), None), check_vma=False
    )
```

```python
import functools

import jax
import jax.numpy as jnp
from jax import lax
from jax.sharding import PartitionSpec as P
from jax.experimental import pallas as pl
from jax.experimental.pallas import tpu as pltpu

HEAD_DIM = 128
GROUP = 1024
MOST = 3


ROTARY_BASE = 10000.0
EPSILON = 1e-05
MASKED = -1e30


def from_behind(x, axis, by):
    length = lax.axis_size(axis)
    pairs = [(i, i + by) for i in range(length) if 0 <= i + by < length]
    return lax.ppermute(x, axis, pairs)


def frequencies(half_dim):
    indices = jnp.arange(half_dim, dtype=jnp.float32)
    return jnp.exp(indices * (-jnp.log(jnp.float32(ROTARY_BASE)) / half_dim))


def rotation_tables(angles, width):
    cosine = jnp.cos(angles)
    sine_part = jnp.sin(angles)
    repeats = width // (2 * angles.shape[-1])
    cos_full = jnp.tile(jnp.concatenate([cosine, cosine], axis=-1), (1, repeats))
    sin_full = jnp.tile(jnp.concatenate([-sine_part, sine_part], axis=-1), (1, repeats))
    return cos_full, sin_full


def rotate_flat(vectors, cos_full, sin_full):
    half_dim = HEAD_DIM // 2
    width = vectors.shape[-1]
    column = jnp.arange(width, dtype=jnp.int32) % HEAD_DIM
    partner = jnp.where(
        (column < half_dim)[None, :],
        jnp.roll(vectors, -half_dim, axis=1),
        jnp.roll(vectors, half_dim, axis=1),
    )
    return vectors * cos_full + partner * sin_full


def group_layout(request_lengths, group_order):
    group_count = group_order.shape[0]
    request_ends = jnp.cumsum(request_lengths)
    group_ids = jnp.arange(group_count, dtype=jnp.int32)
    group_request = jnp.sum((group_ids[:, None] >= request_ends[None, :]).astype(jnp.int32), axis=1)
    same_request = group_request[:, None] == group_request[None, :]
    earlier = group_order[None, :] < group_order[:, None]
    group_rank = jnp.sum((same_request & earlier).astype(jnp.int32), axis=1)
    return (group_request, group_rank)


def layer_norm(rows_in):
    values32 = rows_in.astype(jnp.float32)
    row_mean = jnp.mean(values32, axis=1, keepdims=True)
    centered = values32 - row_mean
    variance = jnp.mean(centered * centered, axis=1, keepdims=True)
    return (centered * lax.rsqrt(variance + EPSILON)).astype(jnp.bfloat16)


def attend(queries, joined_keys, joined_values, visible):
    row_count = queries.shape[0]
    key_count = joined_keys.shape[0]
    head_count = queries.shape[1] // HEAD_DIM
    query_heads = queries.reshape(row_count, head_count, HEAD_DIM)
    key_heads = joined_keys.reshape(key_count, head_count, HEAD_DIM)
    value_heads = joined_values.reshape(key_count, head_count, HEAD_DIM)
    scores = jnp.einsum(
        "qhd,khd->hqk", query_heads, key_heads, preferred_element_type=jnp.float32
    ) * HEAD_DIM ** (-0.5)
    if visible is not None:
        scores = jnp.where(visible[None], scores, MASKED)
    row_max = jnp.max(scores, axis=2)
    weights = jnp.exp(scores - row_max[:, :, None])
    if visible is not None:
        weights = jnp.where(visible[None], weights, 0.0)
    denominator = jnp.sum(weights, axis=2)
    numerator = jnp.einsum(
        "hqk,khd->qhd",
        weights.astype(jnp.bfloat16),
        value_heads,
        preferred_element_type=jnp.float32,
    )
    return (numerator, row_max, denominator)


def combine(first, second):
    row_max = jnp.maximum(first[1], second[1])
    scale_first = jnp.exp(first[1] - row_max)
    scale_second = jnp.exp(second[1] - row_max)
    numerator = (
        first[0] * jnp.transpose(scale_first)[:, :, None]
        + second[0] * jnp.transpose(scale_second)[:, :, None]
    )
    denominator = first[2] * scale_first + second[2] * scale_second
    return (numerator, row_max, denominator)


def own_attention_kernel(index_ref, query_ref, own_key_ref, own_value_ref, max_ref, sum_ref, acc_ref):
    scale = HEAD_DIM ** (-0.5)
    scores = (
        lax.dot_general(
            query_ref[...], own_key_ref[...], (((1,), (1,)), ((), ())),
            preferred_element_type=jnp.float32,
        )
        * scale
    )
    key_ids = lax.broadcasted_iota(jnp.int32, scores.shape, 1)
    visible = key_ids <= index_ref[...]
    scores = jnp.where(visible, scores, MASKED)
    row_max = jnp.max(scores, axis=1, keepdims=True)
    weights = jnp.where(visible, jnp.exp(scores - row_max), 0.0)
    max_ref[...] = jnp.broadcast_to(row_max, max_ref.shape)
    sum_ref[...] = jnp.broadcast_to(jnp.sum(weights, axis=1, keepdims=True), sum_ref.shape)
    acc_ref[...] = jnp.dot(
        weights.astype(jnp.bfloat16), own_value_ref[...], preferred_element_type=jnp.float32
    )


def far_attention_kernel(final, flags_ref, query_ref, max_ref, sum_ref, acc_ref, *refs):
    output_count = 1 if final else 3
    far_refs = refs[:-output_count]
    out_refs = refs[-output_count:]
    scale = HEAD_DIM ** (-0.5)
    query = query_ref[...]
    state = (max_ref[:, :1], sum_ref[:, :1], acc_ref[...])
    for slot in range(len(far_refs) // 2):
        key_ref, value_ref = far_refs[2 * slot : 2 * slot + 2]

        def block(carry, key_ref=key_ref, value_ref=value_ref):
            old_max, old_sum, old_acc = carry
            block_scores = (
                lax.dot_general(
                    query, key_ref[...], (((1,), (1,)), ((), ())),
                    preferred_element_type=jnp.float32,
                )
                * scale
            )
            new_max = jnp.maximum(old_max, jnp.max(block_scores, axis=1, keepdims=True))
            keep = jnp.exp(old_max - new_max)
            block_weights = jnp.exp(block_scores - new_max)
            return (
                new_max,
                keep * old_sum + jnp.sum(block_weights, axis=1, keepdims=True),
                keep * old_acc
                + jnp.dot(
                    block_weights.astype(jnp.bfloat16), value_ref[...],
                    preferred_element_type=jnp.float32,
                ),
            )

        state = lax.cond(flags_ref[slot] != 0, block, lambda carry: carry, state)
    if final:
        out_refs[0][...] = (state[2] / state[1]).astype(out_refs[0].dtype)
    else:
        out_refs[0][...] = jnp.broadcast_to(state[0], out_refs[0].shape)
        out_refs[1][...] = jnp.broadcast_to(state[1], out_refs[1].shape)
        out_refs[2][...] = state[2]


def fused_attention(flags, recompute_index, queries, joined_kv, far_parts):
    row_count, feature_width = queries.shape
    head_count = feature_width // HEAD_DIM
    key_count = joined_kv.shape[0]
    params = pltpu.CompilerParams(vmem_limit_bytes=48 * 1024 * 1024)
    head_block = pl.BlockSpec((row_count, HEAD_DIM), lambda h: (0, h))
    state_shape = jax.ShapeDtypeStruct((row_count, feature_width), jnp.float32)
    running = pl.pallas_call(
        own_attention_kernel,
        grid=(head_count,),
        in_specs=[
            pl.BlockSpec((row_count, 1), lambda h: (0, 0)),
            head_block,
            pl.BlockSpec((key_count, HEAD_DIM), lambda h: (0, h)),
            pl.BlockSpec((key_count, HEAD_DIM), lambda h: (0, h + head_count)),
        ],
        out_specs=[head_block, head_block, head_block],
        out_shape=[state_shape, state_shape, state_shape],
        compiler_params=params,
    )(recompute_index.reshape(row_count, 1), queries, joined_kv, joined_kv)

    def column_spec(rows, offset, slot=None):
        if slot is None:
            return pl.BlockSpec((rows, HEAD_DIM), lambda h, flags_ref: (0, h + offset))
        return pl.BlockSpec(
            (rows, HEAD_DIM), lambda h, flags_ref: (0, (h + offset) * flags_ref[slot])
        )

    for part_index, final in ((0, False), (1, True)):
        in_specs = [column_spec(row_count, 0)] * 4
        operands = [queries, *running]
        for slot, parts in enumerate(far_parts):
            part = parts[part_index]
            in_specs += [
                column_spec(part.shape[0], 0, slot),
                column_spec(part.shape[0], head_count, slot),
            ]
            operands += [part, part]
        out_spec = column_spec(row_count, 0)
        grid_spec = pltpu.PrefetchScalarGridSpec(
            num_scalar_prefetch=1,
            grid=(head_count,),
            in_specs=in_specs,
            out_specs=out_spec if final else [out_spec] * 3,
        )
        out_shape = (
            jax.ShapeDtypeStruct((row_count, feature_width), jnp.bfloat16)
            if final
            else [state_shape] * 3
        )
        running = pl.pallas_call(
            functools.partial(far_attention_kernel, final),
            grid_spec=grid_spec,
            out_shape=out_shape,
            compiler_params=params,
        )(flags, *operands)
    return running


def per_device(
    tokens,
    query_weight,
    kv_weight,
    out_weight,
    cached_keys,
    cached_values,
    request_lengths,
    group_order,
    group_offset,
    recompute_index,
):
    feature_width = query_weight.shape[1]
    head_count = feature_width // HEAD_DIM
    half_dim = HEAD_DIM // 2
    group_count = group_order.shape[0]
    tp_size = lax.axis_size("tp")
    device = lax.axis_index("req")
    tp_index = lax.axis_index("tp")
    group_request, group_rank = group_layout(request_lengths, group_order)
    own_request = group_request[device]
    own_rank = group_rank[device]
    weight_pieces = [out_weight]
    for shift in range(1, tp_size):
        pairs = [(peer, (peer + shift) % tp_size) for peer in range(tp_size)]
        weight_pieces.append(lax.ppermute(out_weight, "tp", pairs))
    freq = frequencies(half_dim)
    key_count = cached_keys.shape[0]
    row_count = recompute_index.shape[0]

    rotation = (own_rank * GROUP - group_offset[device]).astype(jnp.float32)
    group_cos, group_sin = rotation_tables((rotation * freq)[None, :], feature_width)
    rotated_keys = rotate_flat(cached_keys.astype(jnp.float32), group_cos, group_sin).astype(
        jnp.bfloat16
    )
    cached_kv = jnp.concatenate([rotated_keys, cached_values], axis=1)

    key_ids = jnp.arange(key_count, dtype=jnp.int32)
    placement = key_ids[:, None] == recompute_index[None, :]
    replaced = jnp.any(placement, axis=1)
    replaced_before = jnp.sum((recompute_index[None, :] < key_ids[:, None]).astype(jnp.int32), axis=1)
    kept_slot = key_ids - replaced_before
    packing = (~replaced)[None, :] & (
        jnp.arange(key_count - row_count, dtype=jnp.int32)[:, None] == kept_slot[None, :]
    )
    kept_kv = jnp.dot(
        packing.astype(jnp.bfloat16), cached_kv, preferred_element_type=jnp.float32
    ).astype(jnp.bfloat16)

    distances = [distance for distance in range(1, MOST)] + [
        -distance for distance in range(1, MOST)
    ]
    far_kept = [from_behind(kept_kv, "req", distance) for distance in distances]

    local_rows = layer_norm(tokens)
    row_pieces = [local_rows]
    for shift in range(1, tp_size):
        pairs = [(peer, (peer + shift) % tp_size) for peer in range(tp_size)]
        row_pieces.append(lax.ppermute(local_rows, "tp", pairs))
    row_stack = jnp.stack(row_pieces)
    normalized = jnp.concatenate(
        [row_stack[(tp_index - peer) % tp_size] for peer in range(tp_size)], axis=0
    )
    query_part = jnp.dot(normalized, query_weight, preferred_element_type=jnp.float32)
    kv_part = jnp.einsum("nd,dkc->knc", normalized, kv_weight, preferred_element_type=jnp.float32)
    key_part = kv_part[0]
    value_part = kv_part[1]
    positions = (own_rank * GROUP + recompute_index).astype(jnp.float32)
    row_cos, row_sin = rotation_tables(positions[:, None] * freq[None, :], feature_width)
    queries = rotate_flat(query_part, row_cos, row_sin).astype(jnp.bfloat16)
    fresh_keys = rotate_flat(key_part, row_cos, row_sin).astype(jnp.bfloat16)
    fresh_values = value_part.astype(jnp.bfloat16)
    fresh_kv = jnp.concatenate([fresh_keys, fresh_values], axis=1)
    far_fresh = [from_behind(fresh_kv, "req", distance) for distance in distances]

    placed_kv = jnp.dot(
        placement.astype(jnp.bfloat16), fresh_kv, preferred_element_type=jnp.float32
    ).astype(jnp.bfloat16)
    joined_kv = jnp.where(replaced[:, None], placed_kv, cached_kv)
    flags = []
    for distance in distances:
        source_index = jnp.clip(device - distance, 0, group_count - 1)
        source_inside = (device - distance >= 0) & (device - distance < group_count)
        needed = (
            source_inside
            & (group_request[source_index] == own_request)
            & (group_rank[source_index] < own_rank)
        )
        flags.append(needed.astype(jnp.int32))
    attention = fused_attention(
        jnp.stack(flags), recompute_index, queries, joined_kv, list(zip(far_kept, far_fresh))
    )

    chunk = row_count // tp_size

    def rows_for(peer):
        return lax.dynamic_slice_in_dim(attention, peer * chunk, chunk, 0)

    mixed = jnp.dot(rows_for(tp_index), weight_pieces[0], preferred_element_type=jnp.float32)
    for shift in range(1, tp_size):
        pairs = [(peer, (peer + shift) % tp_size) for peer in range(tp_size)]
        arrived = lax.ppermute(rows_for((tp_index + shift) % tp_size), "tp", pairs)
        mixed = mixed + jnp.dot(arrived, weight_pieces[shift], preferred_element_type=jnp.float32)
    return mixed.astype(jnp.bfloat16)


def solution(mesh):
    placed = (
        P(("req", "tp"), None),
        P(None, "tp"),
        P(None, None, "tp"),
        P("tp", None),
        P("req", "tp"),
        P("req", "tp"),
        P(),
        P(),
        P(),
        P("req"),
    )
    return jax.shard_map(
        per_device, mesh=mesh, in_specs=placed, out_specs=P(("req", "tp"), None), check_vma=False
    )
```

```python
import functools

import jax
import jax.numpy as jnp
from jax import lax
from jax.sharding import PartitionSpec as P
from jax.experimental import pallas as pl
from jax.experimental.pallas import tpu as pltpu

HEAD_DIM = 128
GROUP = 1024
MOST = 3


ROTARY_BASE = 10000.0
EPSILON = 1e-05
MASKED = -1e30


def from_behind(x, axis, by):
    length = lax.axis_size(axis)
    pairs = [(i, i + by) for i in range(length) if 0 <= i + by < length]
    return lax.ppermute(x, axis, pairs)


def frequencies(half_dim):
    indices = jnp.arange(half_dim, dtype=jnp.float32)
    return jnp.exp(indices * (-jnp.log(jnp.float32(ROTARY_BASE)) / half_dim))


def rotation_tables(angles, width):
    cosine = jnp.cos(angles)
    sine_part = jnp.sin(angles)
    repeats = width // (2 * angles.shape[-1])
    cos_full = jnp.tile(jnp.concatenate([cosine, cosine], axis=-1), (1, repeats))
    sin_full = jnp.tile(jnp.concatenate([-sine_part, sine_part], axis=-1), (1, repeats))
    return cos_full, sin_full


def rotate_flat(vectors, cos_full, sin_full):
    half_dim = HEAD_DIM // 2
    width = vectors.shape[-1]
    column = jnp.arange(width, dtype=jnp.int32) % HEAD_DIM
    partner = jnp.where(
        (column < half_dim)[None, :],
        jnp.roll(vectors, -half_dim, axis=1),
        jnp.roll(vectors, half_dim, axis=1),
    )
    return vectors * cos_full + partner * sin_full


def group_layout(request_lengths, group_order):
    group_count = group_order.shape[0]
    request_ends = jnp.cumsum(request_lengths)
    group_ids = jnp.arange(group_count, dtype=jnp.int32)
    group_request = jnp.sum((group_ids[:, None] >= request_ends[None, :]).astype(jnp.int32), axis=1)
    same_request = group_request[:, None] == group_request[None, :]
    earlier = group_order[None, :] < group_order[:, None]
    group_rank = jnp.sum((same_request & earlier).astype(jnp.int32), axis=1)
    return (group_request, group_rank)


def layer_norm(rows_in):
    values32 = rows_in.astype(jnp.float32)
    row_mean = jnp.mean(values32, axis=1, keepdims=True)
    centered = values32 - row_mean
    variance = jnp.mean(centered * centered, axis=1, keepdims=True)
    return (centered * lax.rsqrt(variance + EPSILON)).astype(jnp.bfloat16)


def attend(queries, joined_keys, joined_values, visible):
    row_count = queries.shape[0]
    key_count = joined_keys.shape[0]
    head_count = queries.shape[1] // HEAD_DIM
    query_heads = queries.reshape(row_count, head_count, HEAD_DIM)
    key_heads = joined_keys.reshape(key_count, head_count, HEAD_DIM)
    value_heads = joined_values.reshape(key_count, head_count, HEAD_DIM)
    scores = jnp.einsum(
        "qhd,khd->hqk", query_heads, key_heads, preferred_element_type=jnp.float32
    ) * HEAD_DIM ** (-0.5)
    if visible is not None:
        scores = jnp.where(visible[None], scores, MASKED)
    row_max = jnp.max(scores, axis=2)
    weights = jnp.exp(scores - row_max[:, :, None])
    if visible is not None:
        weights = jnp.where(visible[None], weights, 0.0)
    denominator = jnp.sum(weights, axis=2)
    numerator = jnp.einsum(
        "hqk,khd->qhd",
        weights.astype(jnp.bfloat16),
        value_heads,
        preferred_element_type=jnp.float32,
    )
    return (numerator, row_max, denominator)


def combine(first, second):
    row_max = jnp.maximum(first[1], second[1])
    scale_first = jnp.exp(first[1] - row_max)
    scale_second = jnp.exp(second[1] - row_max)
    numerator = (
        first[0] * jnp.transpose(scale_first)[:, :, None]
        + second[0] * jnp.transpose(scale_second)[:, :, None]
    )
    denominator = first[2] * scale_first + second[2] * scale_second
    return (numerator, row_max, denominator)


def own_attention_kernel(index_ref, query_ref, own_key_ref, own_value_ref, max_ref, sum_ref, acc_ref):
    scale = HEAD_DIM ** (-0.5)
    scores = (
        lax.dot_general(
            query_ref[...], own_key_ref[...], (((1,), (1,)), ((), ())),
            preferred_element_type=jnp.float32,
        )
        * scale
    )
    key_ids = lax.broadcasted_iota(jnp.int32, scores.shape, 1)
    visible = key_ids <= index_ref[...]
    scores = jnp.where(visible, scores, MASKED)
    row_max = jnp.max(scores, axis=1, keepdims=True)
    weights = jnp.where(visible, jnp.exp(scores - row_max), 0.0)
    max_ref[...] = jnp.broadcast_to(row_max, max_ref.shape)
    sum_ref[...] = jnp.broadcast_to(jnp.sum(weights, axis=1, keepdims=True), sum_ref.shape)
    acc_ref[...] = jnp.dot(
        weights.astype(jnp.bfloat16), own_value_ref[...], preferred_element_type=jnp.float32
    )


def far_attention_kernel(final, flags_ref, query_ref, max_ref, sum_ref, acc_ref, *refs):
    output_count = 1 if final else 3
    far_refs = refs[:-output_count]
    out_refs = refs[-output_count:]
    scale = HEAD_DIM ** (-0.5)
    query = query_ref[...]
    state = (max_ref[:, :1], sum_ref[:, :1], acc_ref[...])
    for slot in range(len(far_refs) // 2):
        key_ref, value_ref = far_refs[2 * slot : 2 * slot + 2]

        def block(carry, key_ref=key_ref, value_ref=value_ref):
            old_max, old_sum, old_acc = carry
            block_scores = (
                lax.dot_general(
                    query, key_ref[...], (((1,), (1,)), ((), ())),
                    preferred_element_type=jnp.float32,
                )
                * scale
            )
            new_max = jnp.maximum(old_max, jnp.max(block_scores, axis=1, keepdims=True))
            keep = jnp.exp(old_max - new_max)
            block_weights = jnp.exp(block_scores - new_max)
            return (
                new_max,
                keep * old_sum + jnp.sum(block_weights, axis=1, keepdims=True),
                keep * old_acc
                + jnp.dot(
                    block_weights.astype(jnp.bfloat16), value_ref[...],
                    preferred_element_type=jnp.float32,
                ),
            )

        state = lax.cond(flags_ref[slot] != 0, block, lambda carry: carry, state)
    if final:
        out_refs[0][...] = (state[2] / state[1]).astype(out_refs[0].dtype)
    else:
        out_refs[0][...] = jnp.broadcast_to(state[0], out_refs[0].shape)
        out_refs[1][...] = jnp.broadcast_to(state[1], out_refs[1].shape)
        out_refs[2][...] = state[2]


def fused_attention(flags, recompute_index, queries, joined_kv, far_parts):
    row_count, feature_width = queries.shape
    head_count = feature_width // HEAD_DIM
    key_count = joined_kv.shape[0]
    params = pltpu.CompilerParams(vmem_limit_bytes=48 * 1024 * 1024)
    head_block = pl.BlockSpec((row_count, HEAD_DIM), lambda h: (0, h))
    state_shape = jax.ShapeDtypeStruct((row_count, feature_width), jnp.float32)
    running = pl.pallas_call(
        own_attention_kernel,
        grid=(head_count,),
        in_specs=[
            pl.BlockSpec((row_count, 1), lambda h: (0, 0)),
            head_block,
            pl.BlockSpec((key_count, HEAD_DIM), lambda h: (0, h)),
            pl.BlockSpec((key_count, HEAD_DIM), lambda h: (0, h + head_count)),
        ],
        out_specs=[head_block, head_block, head_block],
        out_shape=[state_shape, state_shape, state_shape],
        compiler_params=params,
    )(recompute_index.reshape(row_count, 1), queries, joined_kv, joined_kv)

    def column_spec(rows, offset, slot=None):
        if slot is None:
            return pl.BlockSpec((rows, HEAD_DIM), lambda h, flags_ref: (0, h + offset))
        return pl.BlockSpec(
            (rows, HEAD_DIM), lambda h, flags_ref: (0, (h + offset) * flags_ref[slot])
        )

    for part_index, final in ((0, False), (1, True)):
        in_specs = [column_spec(row_count, 0)] * 4
        operands = [queries, *running]
        for slot, parts in enumerate(far_parts):
            part = parts[part_index]
            in_specs += [
                column_spec(part.shape[0], 0, slot),
                column_spec(part.shape[0], head_count, slot),
            ]
            operands += [part, part]
        out_spec = column_spec(row_count, 0)
        grid_spec = pltpu.PrefetchScalarGridSpec(
            num_scalar_prefetch=1,
            grid=(head_count,),
            in_specs=in_specs,
            out_specs=out_spec if final else [out_spec] * 3,
        )
        out_shape = (
            jax.ShapeDtypeStruct((row_count, feature_width), jnp.bfloat16)
            if final
            else [state_shape] * 3
        )
        running = pl.pallas_call(
            functools.partial(far_attention_kernel, final),
            grid_spec=grid_spec,
            out_shape=out_shape,
            compiler_params=params,
        )(flags, *operands)
    return running


def per_device(
    tokens,
    query_weight,
    kv_weight,
    out_weight,
    cached_keys,
    cached_values,
    request_lengths,
    group_order,
    group_offset,
    recompute_index,
):
    feature_width = query_weight.shape[1]
    head_count = feature_width // HEAD_DIM
    half_dim = HEAD_DIM // 2
    group_count = group_order.shape[0]
    tp_size = lax.axis_size("tp")
    device = lax.axis_index("req")
    tp_index = lax.axis_index("tp")
    group_request, group_rank = group_layout(request_lengths, group_order)
    own_request = group_request[device]
    own_rank = group_rank[device]
    core = device % 2
    half_width = out_weight.shape[1] // 2
    weight_half = lax.dynamic_slice_in_dim(out_weight, core * half_width, half_width, 1)
    weight_pieces = [weight_half]
    for shift in range(1, tp_size):
        pairs = [(peer, (peer + shift) % tp_size) for peer in range(tp_size)]
        weight_pieces.append(lax.ppermute(weight_half, "tp", pairs))
    req_size = lax.axis_size("req")
    sibling = [(i, i ^ 1) for i in range(req_size)]
    freq = frequencies(half_dim)
    key_count = cached_keys.shape[0]
    row_count = recompute_index.shape[0]

    rotation = (own_rank * GROUP - group_offset[device]).astype(jnp.float32)
    group_cos, group_sin = rotation_tables((rotation * freq)[None, :], feature_width)
    rotated_keys = rotate_flat(cached_keys.astype(jnp.float32), group_cos, group_sin).astype(
        jnp.bfloat16
    )
    cached_kv = jnp.concatenate([rotated_keys, cached_values], axis=1)

    key_ids = jnp.arange(key_count, dtype=jnp.int32)
    placement = key_ids[:, None] == recompute_index[None, :]
    replaced = jnp.any(placement, axis=1)
    replaced_before = jnp.sum((recompute_index[None, :] < key_ids[:, None]).astype(jnp.int32), axis=1)
    kept_slot = key_ids - replaced_before
    packing = (~replaced)[None, :] & (
        jnp.arange(key_count - row_count, dtype=jnp.int32)[:, None] == kept_slot[None, :]
    )
    kept_kv = jnp.dot(
        packing.astype(jnp.bfloat16), cached_kv, preferred_element_type=jnp.float32
    ).astype(jnp.bfloat16)

    distances = [distance for distance in range(1, MOST)] + [
        -distance for distance in range(1, MOST)
    ]
    far_kept = [from_behind(kept_kv, "req", distance) for distance in distances]

    local_rows = layer_norm(tokens)
    row_pieces = [local_rows]
    for shift in range(1, tp_size):
        pairs = [(peer, (peer + shift) % tp_size) for peer in range(tp_size)]
        row_pieces.append(lax.ppermute(local_rows, "tp", pairs))
    row_stack = jnp.stack(row_pieces)
    normalized = jnp.concatenate(
        [row_stack[(tp_index - peer) % tp_size] for peer in range(tp_size)], axis=0
    )
    query_part = jnp.dot(normalized, query_weight, preferred_element_type=jnp.float32)
    kv_part = jnp.einsum("nd,dkc->knc", normalized, kv_weight, preferred_element_type=jnp.float32)
    key_part = kv_part[0]
    value_part = kv_part[1]
    positions = (own_rank * GROUP + recompute_index).astype(jnp.float32)
    row_cos, row_sin = rotation_tables(positions[:, None] * freq[None, :], feature_width)
    queries = rotate_flat(query_part, row_cos, row_sin).astype(jnp.bfloat16)
    fresh_keys = rotate_flat(key_part, row_cos, row_sin).astype(jnp.bfloat16)
    fresh_values = value_part.astype(jnp.bfloat16)
    fresh_kv = jnp.concatenate([fresh_keys, fresh_values], axis=1)
    far_fresh = [from_behind(fresh_kv, "req", distance) for distance in distances]

    placed_kv = jnp.dot(
        placement.astype(jnp.bfloat16), fresh_kv, preferred_element_type=jnp.float32
    ).astype(jnp.bfloat16)
    joined_kv = jnp.where(replaced[:, None], placed_kv, cached_kv)
    flags = []
    for distance in distances:
        source_index = jnp.clip(device - distance, 0, group_count - 1)
        source_inside = (device - distance >= 0) & (device - distance < group_count)
        needed = (
            source_inside
            & (group_request[source_index] == own_request)
            & (group_rank[source_index] < own_rank)
        )
        flags.append(needed.astype(jnp.int32))
    attention = fused_attention(
        jnp.stack(flags), recompute_index, queries, joined_kv, list(zip(far_kept, far_fresh))
    )

    chunk = row_count // tp_size

    def rows_for(peer):
        return lax.dynamic_slice_in_dim(attention, peer * chunk, chunk, 0)

    own_pieces = [rows_for(tp_index)]
    for shift in range(1, tp_size):
        pairs = [(peer, (peer + shift) % tp_size) for peer in range(tp_size)]
        own_pieces.append(lax.ppermute(rows_for((tp_index + shift) % tp_size), "tp", pairs))
    own_cat = jnp.concatenate(own_pieces, axis=1)
    both_rows = jnp.concatenate([own_cat, lax.ppermute(own_cat, "req", sibling)], axis=0)
    both_mixed = jnp.dot(
        both_rows[:, :feature_width], weight_pieces[0], preferred_element_type=jnp.float32
    )
    for shift in range(1, tp_size):
        both_mixed = both_mixed + jnp.dot(
            both_rows[:, shift * feature_width : (shift + 1) * feature_width],
            weight_pieces[shift],
            preferred_element_type=jnp.float32,
        )
    both_mixed = both_mixed.astype(jnp.bfloat16)
    mixed_mine = both_mixed[:chunk]
    mixed_other = lax.ppermute(both_mixed[chunk:], "req", sibling)
    return jnp.where(
        core == 0,
        jnp.concatenate([mixed_mine, mixed_other], axis=1),
        jnp.concatenate([mixed_other, mixed_mine], axis=1),
    )


def solution(mesh):
    placed = (
        P(("req", "tp"), None),
        P(None, "tp"),
        P(None, None, "tp"),
        P("tp", None),
        P("req", "tp"),
        P("req", "tp"),
        P(),
        P(),
        P(),
        P("req"),
    )
    return jax.shard_map(
        per_device, mesh=mesh, in_specs=placed, out_specs=P(("req", "tp"), None), check_vma=False
    )
```

```python
import functools

import jax
import jax.numpy as jnp
from jax import lax
from jax.sharding import PartitionSpec as P
from jax.experimental import pallas as pl
from jax.experimental.pallas import tpu as pltpu

HEAD_DIM = 128
GROUP = 1024
MOST = 3


ROTARY_BASE = 10000.0
EPSILON = 1e-05
MASKED = -1e30


def from_behind(x, axis, by):
    length = lax.axis_size(axis)
    pairs = [(i, i + by) for i in range(length) if 0 <= i + by < length]
    return lax.ppermute(x, axis, pairs)


def frequencies(half_dim):
    indices = jnp.arange(half_dim, dtype=jnp.float32)
    return jnp.exp(indices * (-jnp.log(jnp.float32(ROTARY_BASE)) / half_dim))


def rotation_tables(angles, width):
    cosine = jnp.cos(angles)
    sine_part = jnp.sin(angles)
    repeats = width // (2 * angles.shape[-1])
    cos_full = jnp.tile(jnp.concatenate([cosine, cosine], axis=-1), (1, repeats))
    sin_full = jnp.tile(jnp.concatenate([-sine_part, sine_part], axis=-1), (1, repeats))
    return cos_full, sin_full


def rotate_flat(vectors, cos_full, sin_full):
    half_dim = HEAD_DIM // 2
    width = vectors.shape[-1]
    column = jnp.arange(width, dtype=jnp.int32) % HEAD_DIM
    partner = jnp.where(
        (column < half_dim)[None, :],
        jnp.roll(vectors, -half_dim, axis=1),
        jnp.roll(vectors, half_dim, axis=1),
    )
    return vectors * cos_full + partner * sin_full


def group_layout(request_lengths, group_order):
    group_count = group_order.shape[0]
    request_ends = jnp.cumsum(request_lengths)
    group_ids = jnp.arange(group_count, dtype=jnp.int32)
    group_request = jnp.sum((group_ids[:, None] >= request_ends[None, :]).astype(jnp.int32), axis=1)
    same_request = group_request[:, None] == group_request[None, :]
    earlier = group_order[None, :] < group_order[:, None]
    group_rank = jnp.sum((same_request & earlier).astype(jnp.int32), axis=1)
    return (group_request, group_rank)


def layer_norm(rows_in):
    values32 = rows_in.astype(jnp.float32)
    row_mean = jnp.mean(values32, axis=1, keepdims=True)
    centered = values32 - row_mean
    variance = jnp.mean(centered * centered, axis=1, keepdims=True)
    return (centered * lax.rsqrt(variance + EPSILON)).astype(jnp.bfloat16)


def own_attention_kernel(index_ref, query_ref, own_key_ref, own_value_ref, max_ref, sum_ref, acc_ref):
    scale = HEAD_DIM ** (-0.5)
    scores = (
        lax.dot_general(
            query_ref[...], own_key_ref[...], (((1,), (1,)), ((), ())),
            preferred_element_type=jnp.float32,
        )
        * scale
    )
    key_ids = lax.broadcasted_iota(jnp.int32, scores.shape, 1)
    visible = key_ids <= index_ref[...]
    scores = jnp.where(visible, scores, MASKED)
    row_max = jnp.max(scores, axis=1, keepdims=True)
    weights = jnp.where(visible, jnp.exp(scores - row_max), 0.0)
    max_ref[...] = jnp.broadcast_to(row_max, max_ref.shape)
    sum_ref[...] = jnp.broadcast_to(jnp.sum(weights, axis=1, keepdims=True), sum_ref.shape)
    acc_ref[...] = jnp.dot(
        weights.astype(jnp.bfloat16), own_value_ref[...], preferred_element_type=jnp.float32
    )


def far_attention_kernel(final, flags_ref, query_ref, max_ref, sum_ref, acc_ref, *refs):
    output_count = 1 if final else 3
    far_refs = refs[:-output_count]
    out_refs = refs[-output_count:]
    scale = HEAD_DIM ** (-0.5)
    query = query_ref[...]
    state = (max_ref[:, :1], sum_ref[:, :1], acc_ref[...])
    for slot in range(len(far_refs) // 2):
        key_ref, value_ref = far_refs[2 * slot : 2 * slot + 2]

        def block(carry, key_ref=key_ref, value_ref=value_ref):
            old_max, old_sum, old_acc = carry
            block_scores = (
                lax.dot_general(
                    query, key_ref[...], (((1,), (1,)), ((), ())),
                    preferred_element_type=jnp.float32,
                )
                * scale
            )
            new_max = jnp.maximum(old_max, jnp.max(block_scores, axis=1, keepdims=True))
            keep = jnp.exp(old_max - new_max)
            block_weights = jnp.exp(block_scores - new_max)
            return (
                new_max,
                keep * old_sum + jnp.sum(block_weights, axis=1, keepdims=True),
                keep * old_acc
                + jnp.dot(
                    block_weights.astype(jnp.bfloat16), value_ref[...],
                    preferred_element_type=jnp.float32,
                ),
            )

        state = lax.cond(flags_ref[slot] != 0, block, lambda carry: carry, state)
    if final:
        out_refs[0][...] = (state[2] / state[1]).astype(out_refs[0].dtype)
    else:
        out_refs[0][...] = jnp.broadcast_to(state[0], out_refs[0].shape)
        out_refs[1][...] = jnp.broadcast_to(state[1], out_refs[1].shape)
        out_refs[2][...] = state[2]


def fused_attention(flags, recompute_index, queries, joined_kv, far_parts):
    row_count, feature_width = queries.shape
    head_count = feature_width // HEAD_DIM
    key_count = joined_kv.shape[0]
    params = pltpu.CompilerParams(vmem_limit_bytes=48 * 1024 * 1024)
    head_block = pl.BlockSpec((row_count, HEAD_DIM), lambda h: (0, h))
    state_shape = jax.ShapeDtypeStruct((row_count, feature_width), jnp.float32)
    running = pl.pallas_call(
        own_attention_kernel,
        grid=(head_count,),
        in_specs=[
            pl.BlockSpec((row_count, 1), lambda h: (0, 0)),
            head_block,
            pl.BlockSpec((key_count, HEAD_DIM), lambda h: (0, h)),
            pl.BlockSpec((key_count, HEAD_DIM), lambda h: (0, h + head_count)),
        ],
        out_specs=[head_block, head_block, head_block],
        out_shape=[state_shape, state_shape, state_shape],
        compiler_params=params,
    )(recompute_index.reshape(row_count, 1), queries, joined_kv, joined_kv)

    def column_spec(rows, offset, slot=None):
        if slot is None:
            return pl.BlockSpec((rows, HEAD_DIM), lambda h, flags_ref: (0, h + offset))
        return pl.BlockSpec(
            (rows, HEAD_DIM), lambda h, flags_ref: (0, (h + offset) * flags_ref[slot])
        )

    for part_index, final in ((0, False), (1, True)):
        in_specs = [column_spec(row_count, 0)] * 4
        operands = [queries, *running]
        for slot, parts in enumerate(far_parts):
            part = parts[part_index]
            in_specs += [
                column_spec(part.shape[0], 0, slot),
                column_spec(part.shape[0], head_count, slot),
            ]
            operands += [part, part]
        out_spec = column_spec(row_count, 0)
        grid_spec = pltpu.PrefetchScalarGridSpec(
            num_scalar_prefetch=1,
            grid=(head_count,),
            in_specs=in_specs,
            out_specs=out_spec if final else [out_spec] * 3,
        )
        out_shape = (
            jax.ShapeDtypeStruct((row_count, feature_width), jnp.bfloat16)
            if final
            else [state_shape] * 3
        )
        running = pl.pallas_call(
            functools.partial(far_attention_kernel, final),
            grid_spec=grid_spec,
            out_shape=out_shape,
            compiler_params=params,
        )(flags, *operands)
    return running


def per_device(
    tokens,
    query_weight,
    kv_weight,
    out_weight,
    cached_keys,
    cached_values,
    request_lengths,
    group_order,
    group_offset,
    recompute_index,
):
    feature_width = query_weight.shape[1]
    half_dim = HEAD_DIM // 2
    group_count = group_order.shape[0]
    tp_size = lax.axis_size("tp")
    device = lax.axis_index("req")
    tp_index = lax.axis_index("tp")
    group_request, group_rank = group_layout(request_lengths, group_order)
    own_request = group_request[device]
    own_rank = group_rank[device]
    weight_pieces = [out_weight]
    for shift in range(1, tp_size):
        pairs = [(peer, (peer + shift) % tp_size) for peer in range(tp_size)]
        weight_pieces.append(lax.ppermute(out_weight, "tp", pairs))
    freq = frequencies(half_dim)
    key_count = cached_keys.shape[0]
    row_count = recompute_index.shape[0]

    rotation = (own_rank * GROUP - group_offset[device]).astype(jnp.float32)
    group_cos, group_sin = rotation_tables((rotation * freq)[None, :], feature_width)
    rotated_keys = rotate_flat(cached_keys.astype(jnp.float32), group_cos, group_sin).astype(
        jnp.bfloat16
    )
    cached_kv = jnp.concatenate([rotated_keys, cached_values], axis=1)

    key_ids = jnp.arange(key_count, dtype=jnp.int32)
    placement = key_ids[:, None] == recompute_index[None, :]
    replaced = jnp.any(placement, axis=1)
    replaced_before = jnp.sum((recompute_index[None, :] < key_ids[:, None]).astype(jnp.int32), axis=1)
    kept_slot = key_ids - replaced_before
    packing = (~replaced)[None, :] & (
        jnp.arange(key_count - row_count, dtype=jnp.int32)[:, None] == kept_slot[None, :]
    )
    kept_kv = jnp.dot(
        packing.astype(jnp.bfloat16), cached_kv, preferred_element_type=jnp.float32
    ).astype(jnp.bfloat16)

    distances = [distance for distance in range(1, MOST)] + [
        -distance for distance in range(1, MOST)
    ]
    far_kept = [from_behind(kept_kv, "req", distance) for distance in distances]

    local_rows = layer_norm(tokens)
    row_pieces = [local_rows]
    for shift in range(1, tp_size):
        pairs = [(peer, (peer + shift) % tp_size) for peer in range(tp_size)]
        row_pieces.append(lax.ppermute(local_rows, "tp", pairs))
    row_stack = jnp.stack(row_pieces)
    normalized = jnp.concatenate(
        [row_stack[(tp_index - peer) % tp_size] for peer in range(tp_size)], axis=0
    )
    query_part = jnp.dot(normalized, query_weight, preferred_element_type=jnp.float32)
    kv_part = jnp.einsum("nd,dkc->knc", normalized, kv_weight, preferred_element_type=jnp.float32)
    key_part = kv_part[0]
    value_part = kv_part[1]
    positions = (own_rank * GROUP + recompute_index).astype(jnp.float32)
    row_cos, row_sin = rotation_tables(positions[:, None] * freq[None, :], feature_width)
    queries = rotate_flat(query_part, row_cos, row_sin).astype(jnp.bfloat16)
    fresh_keys = rotate_flat(key_part, row_cos, row_sin).astype(jnp.bfloat16)
    fresh_values = value_part.astype(jnp.bfloat16)
    fresh_kv = jnp.concatenate([fresh_keys, fresh_values], axis=1)
    far_fresh = [from_behind(fresh_kv, "req", distance) for distance in distances]

    placed_kv = jnp.dot(
        placement.astype(jnp.bfloat16), fresh_kv, preferred_element_type=jnp.float32
    ).astype(jnp.bfloat16)
    joined_kv = jnp.where(replaced[:, None], placed_kv, cached_kv)
    flags = []
    for distance in distances:
        source_index = jnp.clip(device - distance, 0, group_count - 1)
        source_inside = (device - distance >= 0) & (device - distance < group_count)
        needed = (
            source_inside
            & (group_request[source_index] == own_request)
            & (group_rank[source_index] < own_rank)
        )
        flags.append(needed.astype(jnp.int32))
    attention = fused_attention(
        jnp.stack(flags), recompute_index, queries, joined_kv, list(zip(far_kept, far_fresh))
    )

    chunk = row_count // tp_size

    def rows_for(peer):
        return lax.dynamic_slice_in_dim(attention, peer * chunk, chunk, 0)

    pieces = [rows_for(tp_index)]
    for shift in range(1, tp_size):
        pairs = [(peer, (peer + shift) % tp_size) for peer in range(tp_size)]
        pieces.append(lax.ppermute(rows_for((tp_index + shift) % tp_size), "tp", pairs))
    mixed = jnp.dot(
        jnp.concatenate(pieces, axis=1),
        jnp.concatenate(weight_pieces, axis=0),
        preferred_element_type=jnp.float32,
    )
    return mixed.astype(jnp.bfloat16)


def solution(mesh):
    placed = (
        P(("req", "tp"), None),
        P(None, "tp"),
        P(None, None, "tp"),
        P("tp", None),
        P("req", "tp"),
        P("req", "tp"),
        P(),
        P(),
        P(),
        P("req"),
    )

    return jax.shard_map(
        per_device, mesh=mesh, in_specs=placed, out_specs=P(("req", "tp"), None), check_vma=False
    )
```

```python
import functools

import jax
import jax.numpy as jnp
from jax import lax
from jax.sharding import PartitionSpec as P
from jax.experimental import pallas as pl
from jax.experimental.pallas import tpu as pltpu

HEAD_DIM = 128
GROUP = 1024
MOST = 3


ROTARY_BASE = 10000.0
EPSILON = 1e-05
MASKED = -1e30


def from_behind(x, axis, by):
    length = lax.axis_size(axis)
    pairs = [(i, i + by) for i in range(length) if 0 <= i + by < length]
    return lax.ppermute(x, axis, pairs)


def frequencies(half_dim):
    indices = jnp.arange(half_dim, dtype=jnp.float32)
    return jnp.exp(indices * (-jnp.log(jnp.float32(ROTARY_BASE)) / half_dim))


def rotation_tables(angles, width):
    cosine = jnp.cos(angles)
    sine_part = jnp.sin(angles)
    repeats = width // (2 * angles.shape[-1])
    cos_full = jnp.tile(jnp.concatenate([cosine, cosine], axis=-1), (1, repeats))
    sin_full = jnp.tile(jnp.concatenate([-sine_part, sine_part], axis=-1), (1, repeats))
    return cos_full, sin_full


def rotate_flat(vectors, cos_full, sin_full):
    half_dim = HEAD_DIM // 2
    width = vectors.shape[-1]
    column = jnp.arange(width, dtype=jnp.int32) % HEAD_DIM
    partner = jnp.where(
        (column < half_dim)[None, :],
        jnp.roll(vectors, -half_dim, axis=1),
        jnp.roll(vectors, half_dim, axis=1),
    )
    return vectors * cos_full + partner * sin_full


def group_layout(request_lengths, group_order):
    group_count = group_order.shape[0]
    request_ends = jnp.cumsum(request_lengths)
    group_ids = jnp.arange(group_count, dtype=jnp.int32)
    group_request = jnp.sum((group_ids[:, None] >= request_ends[None, :]).astype(jnp.int32), axis=1)
    same_request = group_request[:, None] == group_request[None, :]
    earlier = group_order[None, :] < group_order[:, None]
    group_rank = jnp.sum((same_request & earlier).astype(jnp.int32), axis=1)
    return (group_request, group_rank)


def layer_norm(rows_in):
    values32 = rows_in.astype(jnp.float32)
    row_mean = jnp.mean(values32, axis=1, keepdims=True)
    centered = values32 - row_mean
    variance = jnp.mean(centered * centered, axis=1, keepdims=True)
    return (centered * lax.rsqrt(variance + EPSILON)).astype(jnp.bfloat16)


def own_attention_kernel(index_ref, query_ref, own_key_ref, own_value_ref, max_ref, sum_ref, acc_ref):
    scale = HEAD_DIM ** (-0.5)
    scores = (
        lax.dot_general(
            query_ref[...], own_key_ref[...], (((1,), (1,)), ((), ())),
            preferred_element_type=jnp.float32,
        )
        * scale
    )
    key_ids = lax.broadcasted_iota(jnp.int32, scores.shape, 1)
    visible = key_ids <= index_ref[...]
    scores = jnp.where(visible, scores, MASKED)
    row_max = jnp.max(scores, axis=1, keepdims=True)
    weights = jnp.exp(scores - row_max)
    max_ref[...] = jnp.broadcast_to(row_max, max_ref.shape)
    sum_ref[...] = jnp.broadcast_to(jnp.sum(weights, axis=1, keepdims=True), sum_ref.shape)
    acc_ref[...] = jnp.dot(
        weights.astype(jnp.bfloat16), own_value_ref[...], preferred_element_type=jnp.float32
    )


def far_attention_kernel(final, flags_ref, query_ref, max_ref, sum_ref, acc_ref, *refs):
    output_count = 1 if final else 3
    far_refs = refs[:-output_count]
    out_refs = refs[-output_count:]
    scale = HEAD_DIM ** (-0.5)
    query = query_ref[...]
    state = (max_ref[:, :1], sum_ref[:, :1], acc_ref[...])
    for slot in range(len(far_refs) // 2):
        key_ref, value_ref = far_refs[2 * slot : 2 * slot + 2]

        def block(carry, key_ref=key_ref, value_ref=value_ref):
            old_max, old_sum, old_acc = carry
            block_scores = (
                lax.dot_general(
                    query, key_ref[...], (((1,), (1,)), ((), ())),
                    preferred_element_type=jnp.float32,
                )
                * scale
            )
            new_max = jnp.maximum(old_max, jnp.max(block_scores, axis=1, keepdims=True))
            keep = jnp.exp(old_max - new_max)
            block_weights = jnp.exp(block_scores - new_max)
            return (
                new_max,
                keep * old_sum + jnp.sum(block_weights, axis=1, keepdims=True),
                keep * old_acc
                + jnp.dot(
                    block_weights.astype(jnp.bfloat16), value_ref[...],
                    preferred_element_type=jnp.float32,
                ),
            )

        state = lax.cond(flags_ref[slot] != 0, block, lambda carry: carry, state)
    if final:
        out_refs[0][...] = (state[2] / state[1]).astype(out_refs[0].dtype)
    else:
        out_refs[0][...] = jnp.broadcast_to(state[0], out_refs[0].shape)
        out_refs[1][...] = jnp.broadcast_to(state[1], out_refs[1].shape)
        out_refs[2][...] = state[2]


def fused_attention(flags, recompute_index, queries, joined_kv, far_parts):
    row_count, feature_width = queries.shape
    head_count = feature_width // HEAD_DIM
    key_count = joined_kv.shape[0]
    params = pltpu.CompilerParams(vmem_limit_bytes=48 * 1024 * 1024)
    head_block = pl.BlockSpec((row_count, HEAD_DIM), lambda h: (0, h))
    state_shape = jax.ShapeDtypeStruct((row_count, feature_width), jnp.float32)
    running = pl.pallas_call(
        own_attention_kernel,
        grid=(head_count,),
        in_specs=[
            pl.BlockSpec((row_count, 1), lambda h: (0, 0)),
            head_block,
            pl.BlockSpec((key_count, HEAD_DIM), lambda h: (0, h)),
            pl.BlockSpec((key_count, HEAD_DIM), lambda h: (0, h + head_count)),
        ],
        out_specs=[head_block, head_block, head_block],
        out_shape=[state_shape, state_shape, state_shape],
        compiler_params=params,
    )(recompute_index.reshape(row_count, 1), queries, joined_kv, joined_kv)

    def column_spec(rows, offset, slot=None):
        if slot is None:
            return pl.BlockSpec((rows, HEAD_DIM), lambda h, flags_ref: (0, h + offset))
        return pl.BlockSpec(
            (rows, HEAD_DIM), lambda h, flags_ref: (0, (h + offset) * flags_ref[slot])
        )

    for part_index, final in ((0, False), (1, True)):
        in_specs = [column_spec(row_count, 0)] * 4
        operands = [queries, *running]
        for slot, parts in enumerate(far_parts):
            part = parts[part_index]
            in_specs += [
                column_spec(part.shape[0], 0, slot),
                column_spec(part.shape[0], head_count, slot),
            ]
            operands += [part, part]
        out_spec = column_spec(row_count, 0)
        grid_spec = pltpu.PrefetchScalarGridSpec(
            num_scalar_prefetch=1,
            grid=(head_count,),
            in_specs=in_specs,
            out_specs=out_spec if final else [out_spec] * 3,
        )
        out_shape = (
            jax.ShapeDtypeStruct((row_count, feature_width), jnp.bfloat16)
            if final
            else [state_shape] * 3
        )
        running = pl.pallas_call(
            functools.partial(far_attention_kernel, final),
            grid_spec=grid_spec,
            out_shape=out_shape,
            compiler_params=params,
        )(flags, *operands)
    return running


def per_device(
    tokens,
    query_weight,
    kv_weight,
    out_weight,
    cached_keys,
    cached_values,
    request_lengths,
    group_order,
    group_offset,
    recompute_index,
):
    feature_width = query_weight.shape[1]
    half_dim = HEAD_DIM // 2
    group_count = group_order.shape[0]
    tp_size = lax.axis_size("tp")
    device = lax.axis_index("req")
    tp_index = lax.axis_index("tp")
    group_request, group_rank = group_layout(request_lengths, group_order)
    own_request = group_request[device]
    own_rank = group_rank[device]
    weight_pieces = [out_weight]
    for shift in range(1, tp_size):
        pairs = [(peer, (peer + shift) % tp_size) for peer in range(tp_size)]
        weight_pieces.append(lax.ppermute(out_weight, "tp", pairs))
    freq = frequencies(half_dim)
    key_count = cached_keys.shape[0]
    row_count = recompute_index.shape[0]

    rotation = (own_rank * GROUP - group_offset[device]).astype(jnp.float32)
    group_cos, group_sin = rotation_tables((rotation * freq)[None, :], feature_width)
    rotated_keys = rotate_flat(cached_keys.astype(jnp.float32), group_cos, group_sin).astype(
        jnp.bfloat16
    )
    cached_kv = jnp.concatenate([rotated_keys, cached_values], axis=1)

    key_ids = jnp.arange(key_count, dtype=jnp.int32)
    placement = key_ids[:, None] == recompute_index[None, :]
    replaced = jnp.any(placement, axis=1)
    replaced_before = jnp.sum((recompute_index[None, :] < key_ids[:, None]).astype(jnp.int32), axis=1)
    kept_slot = key_ids - replaced_before
    packing = (~replaced)[None, :] & (
        jnp.arange(key_count - row_count, dtype=jnp.int32)[:, None] == kept_slot[None, :]
    )
    kept_kv = jnp.dot(
        packing.astype(jnp.bfloat16), cached_kv, preferred_element_type=jnp.float32
    ).astype(jnp.bfloat16)

    distances = [distance for distance in range(1, MOST)] + [
        -distance for distance in range(1, MOST)
    ]
    far_kept = [from_behind(kept_kv, "req", distance) for distance in distances]

    local_rows = layer_norm(tokens)
    row_pieces = [local_rows]
    for shift in range(1, tp_size):
        pairs = [(peer, (peer + shift) % tp_size) for peer in range(tp_size)]
        row_pieces.append(lax.ppermute(local_rows, "tp", pairs))
    row_stack = jnp.stack(row_pieces)
    normalized = jnp.concatenate(
        [row_stack[(tp_index - peer) % tp_size] for peer in range(tp_size)], axis=0
    )
    query_part = jnp.dot(normalized, query_weight, preferred_element_type=jnp.float32)
    kv_part = jnp.einsum("nd,dkc->knc", normalized, kv_weight, preferred_element_type=jnp.float32)
    key_part = kv_part[0]
    value_part = kv_part[1]
    positions = (own_rank * GROUP + recompute_index).astype(jnp.float32)
    row_cos, row_sin = rotation_tables(positions[:, None] * freq[None, :], feature_width)
    queries = rotate_flat(query_part, row_cos, row_sin).astype(jnp.bfloat16)
    fresh_keys = rotate_flat(key_part, row_cos, row_sin).astype(jnp.bfloat16)
    fresh_values = value_part.astype(jnp.bfloat16)
    fresh_kv = jnp.concatenate([fresh_keys, fresh_values], axis=1)
    far_fresh = [from_behind(fresh_kv, "req", distance) for distance in distances]

    placed_kv = jnp.dot(
        placement.astype(jnp.bfloat16), fresh_kv, preferred_element_type=jnp.float32
    ).astype(jnp.bfloat16)
    joined_kv = jnp.where(replaced[:, None], placed_kv, cached_kv)
    flags = []
    for distance in distances:
        source_index = jnp.clip(device - distance, 0, group_count - 1)
        source_inside = (device - distance >= 0) & (device - distance < group_count)
        needed = (
            source_inside
            & (group_request[source_index] == own_request)
            & (group_rank[source_index] < own_rank)
        )
        flags.append(needed.astype(jnp.int32))
    attention = fused_attention(
        jnp.stack(flags), recompute_index, queries, joined_kv, list(zip(far_kept, far_fresh))
    )

    chunk = row_count // tp_size

    def rows_for(peer):
        return lax.dynamic_slice_in_dim(attention, peer * chunk, chunk, 0)

    mixed = jnp.dot(rows_for(tp_index), weight_pieces[0], preferred_element_type=jnp.float32)
    for shift in range(1, tp_size):
        pairs = [(peer, (peer + shift) % tp_size) for peer in range(tp_size)]
        arrived = lax.ppermute(rows_for((tp_index + shift) % tp_size), "tp", pairs)
        mixed = mixed + jnp.dot(arrived, weight_pieces[shift], preferred_element_type=jnp.float32)
    return mixed.astype(jnp.bfloat16)


def solution(mesh):
    placed = (
        P(("req", "tp"), None),
        P(None, "tp"),
        P(None, None, "tp"),
        P("tp", None),
        P("req", "tp"),
        P("req", "tp"),
        P(),
        P(),
        P(),
        P("req"),
    )

    return jax.shard_map(
        per_device, mesh=mesh, in_specs=placed, out_specs=P(("req", "tp"), None), check_vma=False
    )
```
